512 devices in a mesh: dp: 64 (over y, z), tx: 2 (over core), ty: 4 (over x).
Axes of the slice: x: 4, y: 8, z: 8, core: 2. Of those that a mesh axis runs over, the one named last changes fastest.
Arguments:
- tokens: bfloat16 [32768, 2048], P('dp', 'tx'), may hold values from -6 to 6
- query_weight: bfloat16 [2048, 4, 512], P(None, 'ty', 'tx'), may hold values from -0.25 to 0.25
- key_value_weight: bfloat16 [2048, 4, 128], P(None, 'ty'), may hold values from -0.125 to 0.125
- output_weight: bfloat16 [4, 512, 2048], P('ty', 'tx'), may hold values from -0.5 to 0.5
- cache: bfloat16 [64, 4, 2048, 128], P('dp', 'ty'), may hold values from -300 to 300
- lengths: int32 [64], replicated, may hold values from 0 to 8192, as said below
- offsets: int32 [64], replicated, may hold values from 0 to 2047
- slots: int32 [64], replicated, may hold values from 0 to 63, each once
Outputs:
- mixed: bfloat16 [32768, 2048], P('dp', ('tx', 'ty'))
- new_cache: bfloat16 [64, 4, 2048, 128], P('dp', 'ty')
The draws below stay inside these ranges and needn't reach their ends.
Inputs may be any that keep to these rules, and one draw needn't show every extreme that they name: `lengths`: some request has exactly 8192 cached positions. `slots`: every slot belongs to exactly one request.
All inputs are finite; a program needn't handle non-finite values.
Results may differ from the reference program's by a relative error of at most 0.012.
The reference program's roundings to bfloat16 on the way count: a program that leaves them out, or rounds other values in their place, can miss the bound.
Values may be sent and summed in bfloat16 or wider, within the bound.
No kernel may reach another device: no remote copies, remote signals or barrier semaphores. Data moves between devices by JAX's collectives and lax.ppermute only.
A program may use at most 64 MiB of HBM per device.

```python
import math
import jax
import jax.numpy as jnp
from jax import lax

MODEL_WIDTH = 2048
QUERY_HEADS = 32
KEY_VALUE_HEADS = 4
HEAD_SIZE = 64
WINDOW_LENGTH = 2048
MAXLEN = 8192
FRESH_TOKENS = 512
QUERY_PER_KV = 8
REQUEST_COUNT = 64
TOKENS = 32768


def draw_cache(key, part):
    rotary_base = jnp.clip(jax.random.normal(key, (REQUEST_COUNT, KEY_VALUE_HEADS, WINDOW_LENGTH, 2 * HEAD_SIZE), jnp.float32), -6.0, 6.0)
    return rotary_base.astype(jnp.bfloat16)


def draw_lengths(key, part):
    first_random_key, second_random_key = jax.random.split(key)
    drawn = jax.random.randint(first_random_key, (REQUEST_COUNT,), 0, 1025)
    cubed = drawn * drawn // 1024 * drawn
    counts = cubed // (1048576 // MAXLEN)
    chosen = jax.random.randint(second_random_key, (), 0, REQUEST_COUNT)
    return jnp.where(jnp.arange(REQUEST_COUNT) == chosen, MAXLEN, counts).astype(jnp.int32)


def with_ends(array, own_key, least, high):
    dims = array.shape
    spot = [jax.random.randint(jax.random.fold_in(own_key, axis), (), 0, dims[axis]) for axis in range(len(dims))]
    array = array.at[tuple(spot)].set(least)
    longest = dims.index(max(dims))
    spot[longest] = (spot[longest] + 1) % dims[longest]
    return array.at[tuple(spot)].set(high)


def block_scale(rng, dims, shards, smallest, top_value):
    loudness = 1.0
    for dim, parts in shards:
        steps = jax.random.uniform(jax.random.fold_in(jax.random.fold_in(rng, 6), dim), (parts,), jnp.float32, smallest / len(shards), top_value / len(shards))
        loudness = loudness * jnp.repeat(jnp.exp(steps), dims[dim] // parts).reshape((-1,) + (1,) * (len(dims) - 1 - dim))
    return loudness


def centred(own_key, shape, deviation, bound, cuts=(), held_as=jnp.bfloat16):
    level = block_scale(own_key, shape, cuts, -0.22, 0.18) if cuts else 1.0
    values = jax.random.normal(own_key, shape, jnp.float32) * deviation * level
    return jnp.minimum(jnp.maximum(values, -bound), bound).astype(held_as)


def setup_inputs(seed: int = 0) -> dict:
    streams_of = jax.random.split(jax.random.key(seed), 9)
    return {
        "tokens": centred(streams_of[0], (TOKENS, MODEL_WIDTH), 1.0, 6.0, ((0, 64), (1, 2))),
        "query_weight": centred(streams_of[1], (MODEL_WIDTH, KEY_VALUE_HEADS, QUERY_PER_KV * HEAD_SIZE), (MODEL_WIDTH // 4) ** -0.5, 0.25, ((1, 4), (2, 2))),
        "key_value_weight": centred(streams_of[2], (MODEL_WIDTH, KEY_VALUE_HEADS, 2 * HEAD_SIZE), MODEL_WIDTH ** -0.5, 0.125, ((1, 4),)),
        "output_weight": centred(streams_of[3], (KEY_VALUE_HEADS, QUERY_PER_KV * HEAD_SIZE, MODEL_WIDTH), (QUERY_HEADS * HEAD_SIZE // 16) ** -0.5, 0.5, ((0, 4), (1, 2))),
        "cache": draw_cache(jax.random.fold_in(streams_of[8], 71), 0),
        "lengths": draw_lengths(jax.random.fold_in(streams_of[8], 71), 0),
        "offsets": with_ends(jax.random.randint(streams_of[6], (REQUEST_COUNT,), 0, WINDOW_LENGTH), jax.random.fold_in(streams_of[6], 1), 0, WINDOW_LENGTH - 1).astype(jnp.int32),
        "slots": jax.random.permutation(streams_of[7], REQUEST_COUNT).astype(jnp.int32),
    }


EPS = 1e-05

def apply_rotary(values, token_positions):
    width = values.shape[-1]
    half_width = width // 2
    freqs = jnp.exp(jnp.arange(half_width, dtype=jnp.float32) * (-2.0 * math.log(10000.0) / width))
    angles = token_positions.astype(jnp.float32)[:, None] * freqs[None, :]
    cosine = jnp.cos(angles)[:, None, :]
    sine = jnp.sin(angles)[:, None, :]
    leading = values[..., :half_width]
    trailing = values[..., half_width:]
    return jnp.concatenate([leading * cosine - trailing * sine, trailing * cosine + leading * sine], axis=-1)

def reference(tokens, query_weight, key_value_weight, output_weight, cache, lengths, offsets, slots):
    floats = tokens.astype(jnp.float32)
    normalized_input = (floats * lax.rsqrt(lax.optimization_barrier(jnp.mean(floats * floats, axis=1, keepdims=True)) + EPS)).astype(jnp.bfloat16)
    queries = jnp.dot(normalized_input, query_weight.reshape(MODEL_WIDTH, QUERY_HEADS * HEAD_SIZE), preferred_element_type=jnp.float32)
    rotation_pairs = jnp.dot(normalized_input, key_value_weight.reshape(MODEL_WIDTH, KEY_VALUE_HEADS * 2 * HEAD_SIZE), preferred_element_type=jnp.float32)
    queries = queries.reshape(REQUEST_COUNT, FRESH_TOKENS, QUERY_HEADS, HEAD_SIZE)
    rotation_pairs = rotation_pairs.reshape(REQUEST_COUNT, FRESH_TOKENS, KEY_VALUE_HEADS, 2 * HEAD_SIZE)
    factor = 1.0 / math.sqrt(HEAD_SIZE)

    def attend(inputs):
        query_rows, pair, length, offset, slot = inputs
        token_positions = length + jnp.arange(FRESH_TOKENS, dtype=jnp.int32)
        query_rotated = apply_rotary(query_rows, token_positions).astype(jnp.bfloat16).reshape(FRESH_TOKENS, KEY_VALUE_HEADS, QUERY_PER_KV, HEAD_SIZE)
        new_keys = apply_rotary(pair[:, :, :HEAD_SIZE], token_positions).astype(jnp.bfloat16)
        new_values = pair[:, :, HEAD_SIZE:].astype(jnp.bfloat16)
        stored = lax.dynamic_index_in_dim(cache, slot, 0, keepdims=False)
        cycle = jnp.arange(WINDOW_LENGTH, dtype=jnp.int32)
        held = length - 1 - jnp.mod(offset - 1 - cycle, WINDOW_LENGTH)
        cache_mask = (held[None, :] >= 0) & (held[None, :] > token_positions[:, None] - WINDOW_LENGTH)
        rows = jnp.arange(FRESH_TOKENS, dtype=jnp.int32)
        new_mask = rows[None, :] <= rows[:, None]
        mask = jnp.concatenate([cache_mask, new_mask], axis=1)
        keys = jnp.concatenate([stored[:, :, :HEAD_SIZE], jnp.transpose(new_keys, (1, 0, 2))], axis=1)
        values = jnp.concatenate([stored[:, :, HEAD_SIZE:], jnp.transpose(new_values, (1, 0, 2))], axis=1)
        scores = jnp.einsum('qgjd,gkd->gjqk', query_rotated.astype(jnp.float32), keys.astype(jnp.float32)) * factor
        scores = jnp.where(mask[None, None], scores, -jnp.inf)
        top = lax.optimization_barrier(jnp.max(scores, axis=-1, keepdims=True))
        powers = jnp.exp(scores - top)
        total = lax.optimization_barrier(jnp.sum(powers, axis=-1, keepdims=True))
        weights = powers.astype(jnp.bfloat16)
        summed = jnp.einsum('gjqk,gkd->qgjd', weights.astype(jnp.float32), values.astype(jnp.float32))
        attended = (summed / jnp.transpose(total, (2, 0, 1, 3))).astype(jnp.bfloat16)
        entry = jnp.concatenate([new_keys, new_values], axis=-1)
        return (attended.reshape(FRESH_TOKENS, QUERY_HEADS * HEAD_SIZE), entry)
    attended, entries = lax.map(attend, (queries, rotation_pairs, lengths, offsets, slots))
    mixed = jnp.dot(attended.reshape(TOKENS, QUERY_HEADS * HEAD_SIZE), output_weight.reshape(QUERY_HEADS * HEAD_SIZE, MODEL_WIDTH), preferred_element_type=jnp.float32).astype(jnp.bfloat16)
    cycle_rows = jnp.mod(offsets[:, None] + jnp.arange(FRESH_TOKENS, dtype=jnp.int32)[None, :], WINDOW_LENGTH)
    turned = jnp.transpose(cache, (0, 2, 1, 3))
    turned = turned.at[slots[:, None], cycle_rows].set(entries)
    new_cache = jnp.transpose(turned, (0, 2, 1, 3))
    return (mixed, new_cache)
```

```python
import math

import jax
import jax.numpy as jnp
from jax import lax
from jax.sharding import PartitionSpec as P

HEAD_SIZE = 64
WINDOW_LENGTH = 2048


EPS = 1e-05


def apply_rotary(values, token_positions):
    width = values.shape[-1]
    half_width = width // 2
    freqs = jnp.exp(jnp.arange(half_width, dtype=jnp.float32) * (-2.0 * math.log(10000.0) / width))
    angles = token_positions.astype(jnp.float32)[:, None] * freqs[None, :]
    cosine = jnp.cos(angles)[:, None, :]
    sine = jnp.sin(angles)[:, None, :]
    leading = values[..., :half_width]
    trailing = values[..., half_width:]
    return jnp.concatenate(
        [leading * cosine - trailing * sine, trailing * cosine + leading * sine], axis=-1
    )


def carry_in(window):
    return lax.all_to_all(window, "dp", split_axis=0, concat_axis=0, tiled=True)


def carry_out(window):
    return lax.all_to_all(window, "dp", split_axis=0, concat_axis=0, tiled=True)


def reorder(window, order, groups):
    columns = window.shape[1]
    blocks = window.reshape(groups, window.shape[0] // groups, columns)
    return jnp.take(blocks, order, axis=0).reshape(window.shape[0], columns)


def per_device(
    tokens, query_weight, key_value_weight, output_weight, cache, lengths, offsets, slots
):
    request = lax.axis_index("dp")
    groups = lax.axis_size("dp")
    whole = lax.all_gather(tokens, "tx", axis=1, tiled=True)
    rows_new = whole.shape[0]
    width = whole.shape[1]
    floats = whole.astype(jnp.float32)
    normalized_input = (
        floats * lax.rsqrt(jnp.mean(floats * floats, axis=1, keepdims=True) + EPS)
    ).astype(jnp.bfloat16)
    owners = jnp.arange(slots.shape[0], dtype=jnp.int32)
    inverse = jnp.sum(jnp.where(slots[None, :] == owners[:, None], owners[None, :], 0), axis=1)
    stored = cache[0, 0]
    halves = lax.axis_size("tx")
    half_rows = stored.shape[0] // halves
    mine = lax.dynamic_slice_in_dim(stored, lax.axis_index("tx") * half_rows, half_rows, axis=0)
    spread_in = carry_in(mine)
    window_part = carry_in(reorder(spread_in, slots, groups))
    window = lax.all_gather(window_part, "tx", axis=0, tiled=True)
    query_cols = query_weight.shape[2]
    heads = query_cols // HEAD_SIZE
    queries = jnp.dot(
        normalized_input,
        query_weight.reshape(width, query_cols),
        preferred_element_type=jnp.float32,
    )
    rotation_pairs = jnp.dot(
        normalized_input,
        key_value_weight.reshape(width, 2 * HEAD_SIZE),
        preferred_element_type=jnp.float32,
    )
    length = lengths[request]
    offset = offsets[request]
    token_positions = length + jnp.arange(rows_new, dtype=jnp.int32)
    query_rotated = apply_rotary(
        queries.reshape(rows_new, heads, HEAD_SIZE), token_positions
    ).astype(jnp.bfloat16)
    new_keys = apply_rotary(rotation_pairs[:, None, :HEAD_SIZE], token_positions)[:, 0].astype(
        jnp.bfloat16
    )
    new_values = rotation_pairs[:, HEAD_SIZE:].astype(jnp.bfloat16)
    factor = 1.0 / math.sqrt(HEAD_SIZE)
    rows = jnp.arange(rows_new, dtype=jnp.int32)
    new_mask = rows[None, :] <= rows[:, None]
    cycle = jnp.arange(WINDOW_LENGTH, dtype=jnp.int32)
    held = length - 1 - jnp.mod(offset - 1 - cycle, WINDOW_LENGTH)
    cache_mask = (held[None, :] >= 0) & (held[None, :] > token_positions[:, None] - WINDOW_LENGTH)
    mask_all = jnp.concatenate([cache_mask, new_mask], axis=1)
    keys_all = jnp.concatenate([window[:, :HEAD_SIZE], new_keys], axis=0)
    values_all = jnp.concatenate([window[:, HEAD_SIZE:], new_values], axis=0)

    def one_head(query_rows):
        scores = (
            jnp.einsum("qd,kd->qk", query_rows, keys_all, preferred_element_type=jnp.float32)
            * factor
        )
        scores = jnp.where(mask_all, scores, -jnp.inf)
        top = jnp.max(scores, axis=1, keepdims=True)
        powers = jnp.exp(scores - top)
        total = jnp.sum(powers, axis=1, keepdims=True)
        weights = powers.astype(jnp.bfloat16)
        summed = jnp.dot(weights, values_all, preferred_element_type=jnp.float32)
        return (summed / total).astype(jnp.bfloat16)

    outputs = lax.map(one_head, jnp.transpose(query_rotated, (1, 0, 2)))
    attended = jnp.transpose(outputs, (1, 0, 2)).reshape(rows_new, heads * HEAD_SIZE)
    entry = jnp.concatenate([new_keys, new_values], axis=1)
    spread_out = carry_out(entry)
    arrived = carry_out(reorder(spread_out, inverse, groups))
    own_offset = offsets[inverse[request]]
    rolled = jnp.roll(stored, -own_offset, axis=0)
    updated = jnp.roll(jnp.concatenate([arrived, rolled[rows_new:]], axis=0), own_offset, axis=0)
    new_cache = updated[None, None]
    out_rows = output_weight.reshape(output_weight.shape[1], width)
    partial_value = jnp.dot(attended, out_rows, preferred_element_type=jnp.float32)
    summed_out = lax.psum_scatter(partial_value, ("tx", "ty"), scatter_dimension=1, tiled=True)
    mixed = summed_out.astype(jnp.bfloat16)
    return (mixed, new_cache)


def solution(mesh):
    return jax.shard_map(
        per_device,
        mesh=mesh,
        in_specs=(
            P("dp", "tx"),
            P(None, "ty", "tx"),
            P(None, "ty", None),
            P("ty", "tx", None),
            P("dp", "ty", None, None),
            P(),
            P(),
            P(),
        ),
        out_specs=(P("dp", ("tx", "ty")), P("dp", "ty", None, None)),
        check_vma=False,
    )
```

```python
import math

import jax
import jax.numpy as jnp
from jax import lax
from jax.sharding import PartitionSpec as P

HEAD_SIZE = 64
WINDOW_LENGTH = 2048


EPS = 1e-05


def apply_rotary(values, token_positions):
    width = values.shape[-1]
    half_width = width // 2
    freqs = jnp.exp(jnp.arange(half_width, dtype=jnp.float32) * (-2.0 * math.log(10000.0) / width))
    angles = token_positions.astype(jnp.float32)[:, None] * freqs[None, :]
    cosine = jnp.cos(angles)[:, None, :]
    sine = jnp.sin(angles)[:, None, :]
    leading = values[..., :half_width]
    trailing = values[..., half_width:]
    return jnp.concatenate(
        [leading * cosine - trailing * sine, trailing * cosine + leading * sine], axis=-1
    )


def carry_in(window):
    return lax.all_to_all(window, "dp", split_axis=0, concat_axis=0, tiled=True)


def carry_out(window):
    return lax.all_to_all(window, "dp", split_axis=0, concat_axis=0, tiled=True)


def reorder(window, order, groups):
    columns = window.shape[1]
    blocks = window.reshape(groups, window.shape[0] // groups, columns)
    return jnp.take(blocks, order, axis=0).reshape(window.shape[0], columns)


def per_device(
    tokens, query_weight, key_value_weight, output_weight, cache, lengths, offsets, slots
):
    request = lax.axis_index("dp")
    groups = lax.axis_size("dp")
    whole = lax.all_gather(tokens, "tx", axis=1, tiled=True)
    rows_new = whole.shape[0]
    width = whole.shape[1]
    floats = whole.astype(jnp.float32)
    normalized_input = (
        floats * lax.rsqrt(jnp.mean(floats * floats, axis=1, keepdims=True) + EPS)
    ).astype(jnp.bfloat16)
    owners = jnp.arange(slots.shape[0], dtype=jnp.int32)
    inverse = jnp.sum(jnp.where(slots[None, :] == owners[:, None], owners[None, :], 0), axis=1)
    stored = cache[0, 0]
    halves = lax.axis_size("tx")
    half_rows = stored.shape[0] // halves
    mine = lax.dynamic_slice_in_dim(stored, lax.axis_index("tx") * half_rows, half_rows, axis=0)
    spread_in = carry_in(mine)
    query_cols = query_weight.shape[2]
    heads = query_cols // HEAD_SIZE
    queries = jnp.dot(
        normalized_input,
        query_weight.reshape(width, query_cols),
        preferred_element_type=jnp.float32,
    )
    rotation_pairs = jnp.dot(
        normalized_input,
        key_value_weight.reshape(width, 2 * HEAD_SIZE),
        preferred_element_type=jnp.float32,
    )
    length = lengths[request]
    offset = offsets[request]
    token_positions = length + jnp.arange(rows_new, dtype=jnp.int32)
    query_rotated = apply_rotary(
        queries.reshape(rows_new, heads, HEAD_SIZE), token_positions
    ).astype(jnp.bfloat16)
    new_keys = apply_rotary(rotation_pairs[:, None, :HEAD_SIZE], token_positions)[:, 0].astype(
        jnp.bfloat16
    )
    new_values = rotation_pairs[:, HEAD_SIZE:].astype(jnp.bfloat16)
    entry = jnp.concatenate([new_keys, new_values], axis=1)
    window_chunk = half_rows // groups
    entry_chunk = rows_new // groups
    payload = jnp.concatenate(
        [
            reorder(spread_in, slots, groups).reshape(groups, window_chunk, -1),
            entry.reshape(groups, entry_chunk, -1),
        ],
        axis=1,
    ).reshape(groups * (window_chunk + entry_chunk), -1)
    delivered = carry_in(payload).reshape(groups, window_chunk + entry_chunk, -1)
    window_part = delivered[:, :window_chunk].reshape(half_rows, -1)
    entry_parts = delivered[:, window_chunk:].reshape(rows_new, -1)
    window = lax.all_gather(window_part, "tx", axis=0, tiled=True)
    factor = 1.0 / math.sqrt(HEAD_SIZE)
    rows = jnp.arange(rows_new, dtype=jnp.int32)
    new_mask = rows[None, :] <= rows[:, None]
    cycle = jnp.arange(WINDOW_LENGTH, dtype=jnp.int32)
    held = length - 1 - jnp.mod(offset - 1 - cycle, WINDOW_LENGTH)
    cache_mask = (held[None, :] >= 0) & (held[None, :] > token_positions[:, None] - WINDOW_LENGTH)
    mask_all = jnp.concatenate([cache_mask, new_mask], axis=1)
    keys_all = jnp.concatenate([window[:, :HEAD_SIZE], new_keys], axis=0)
    values_all = jnp.concatenate([window[:, HEAD_SIZE:], new_values], axis=0)

    def one_head(query_rows):
        scores = (
            jnp.einsum("qd,kd->qk", query_rows, keys_all, preferred_element_type=jnp.float32)
            * factor
        )
        scores = jnp.where(mask_all, scores, -jnp.inf)
        top = jnp.max(scores, axis=1, keepdims=True)
        powers = jnp.exp(scores - top)
        total = jnp.sum(powers, axis=1, keepdims=True)
        weights = powers.astype(jnp.bfloat16)
        summed = jnp.dot(weights, values_all, preferred_element_type=jnp.float32)
        return (summed / total).astype(jnp.bfloat16)

    outputs = lax.map(one_head, jnp.transpose(query_rotated, (1, 0, 2)))
    attended = jnp.transpose(outputs, (1, 0, 2)).reshape(rows_new, heads * HEAD_SIZE)
    arrived = carry_out(reorder(entry_parts, inverse, groups))
    own_offset = offsets[inverse[request]]
    rolled = jnp.roll(stored, -own_offset, axis=0)
    updated = jnp.roll(jnp.concatenate([arrived, rolled[rows_new:]], axis=0), own_offset, axis=0)
    new_cache = updated[None, None]
    out_rows = output_weight.reshape(output_weight.shape[1], width)
    partial_value = jnp.dot(attended, out_rows, preferred_element_type=jnp.float32)
    across_cores = lax.psum_scatter(partial_value, "tx", scatter_dimension=1, tiled=True)
    summed_out = lax.psum_scatter(across_cores, "ty", scatter_dimension=1, tiled=True)
    mixed = summed_out.astype(jnp.bfloat16)
    return (mixed, new_cache)


def solution(mesh):
    return jax.shard_map(
        per_device,
        mesh=mesh,
        in_specs=(
            P("dp", "tx"),
            P(None, "ty", "tx"),
            P(None, "ty", None),
            P("ty", "tx", None),
            P("dp", "ty", None, None),
            P(),
            P(),
            P(),
        ),
        out_specs=(P("dp", ("tx", "ty")), P("dp", "ty", None, None)),
        check_vma=False,
    )
```

```python
import math

import jax
import jax.numpy as jnp
from jax import lax
from jax.sharding import PartitionSpec as P

HEAD_SIZE = 64
WINDOW_LENGTH = 2048


EPS = 1e-05


def apply_rotary(values, token_positions):
    width = values.shape[-1]
    half_width = width // 2
    freqs = jnp.exp(jnp.arange(half_width, dtype=jnp.float32) * (-2.0 * math.log(10000.0) / width))
    angles = token_positions.astype(jnp.float32)[:, None] * freqs[None, :]
    cosine = jnp.cos(angles)[:, None, :]
    sine = jnp.sin(angles)[:, None, :]
    leading = values[..., :half_width]
    trailing = values[..., half_width:]
    return jnp.concatenate(
        [leading * cosine - trailing * sine, trailing * cosine + leading * sine], axis=-1
    )


def carry_in(window):
    return lax.all_to_all(window, "dp", split_axis=0, concat_axis=0, tiled=True)


def carry_out(window):
    return lax.all_to_all(window, "dp", split_axis=0, concat_axis=0, tiled=True)


def reorder(window, order, groups):
    columns = window.shape[1]
    blocks = window.reshape(groups, window.shape[0] // groups, columns)
    return jnp.take(blocks, order, axis=0).reshape(window.shape[0], columns)


def per_device(
    tokens, query_weight, key_value_weight, output_weight, cache, lengths, offsets, slots
):
    request = lax.axis_index("dp")
    groups = lax.axis_size("dp")
    halves = lax.axis_size("tx")
    core = lax.axis_index("tx")
    if halves == 2:
        other = lax.ppermute(tokens, "tx", [(0, 1), (1, 0)])
        whole = jnp.where(
            core == 0,
            jnp.concatenate([tokens, other], axis=1),
            jnp.concatenate([other, tokens], axis=1),
        )
    else:
        whole = lax.all_gather(tokens, "tx", axis=1, tiled=True)
    rows_new = whole.shape[0]
    width = whole.shape[1]
    floats = whole.astype(jnp.float32)
    normalized_input = (
        floats * lax.rsqrt(jnp.mean(floats * floats, axis=1, keepdims=True) + EPS)
    ).astype(jnp.bfloat16)
    owners = jnp.arange(slots.shape[0], dtype=jnp.int32)
    inverse = jnp.sum(jnp.where(slots[None, :] == owners[:, None], owners[None, :], 0), axis=1)
    length = lengths[request]
    offset = offsets[request]
    token_positions = length + jnp.arange(rows_new, dtype=jnp.int32)
    rotation_pairs = jnp.dot(
        normalized_input,
        key_value_weight.reshape(width, 2 * HEAD_SIZE),
        preferred_element_type=jnp.float32,
    )
    new_keys = apply_rotary(rotation_pairs[:, None, :HEAD_SIZE], token_positions)[:, 0].astype(
        jnp.bfloat16
    )
    new_values = rotation_pairs[:, HEAD_SIZE:].astype(jnp.bfloat16)
    entry = jnp.concatenate([new_keys, new_values], axis=1)

    stored = cache[0, 0]
    half_rows = stored.shape[0] // halves
    mine = lax.dynamic_slice_in_dim(stored, core * half_rows, half_rows, axis=0)
    window_chunk = half_rows // groups
    entry_chunk = rows_new // groups
    lanes = stored.shape[1]
    first = jnp.concatenate(
        [mine.reshape(groups, window_chunk, lanes), entry.reshape(groups, entry_chunk, lanes)],
        axis=1,
    ).reshape(groups * (window_chunk + entry_chunk), lanes)
    spread = carry_in(first).reshape(groups, window_chunk + entry_chunk, lanes)
    second = jnp.concatenate(
        [
            jnp.take(spread[:, :window_chunk], slots, axis=0),
            jnp.take(spread[:, window_chunk:], inverse, axis=0),
        ],
        axis=1,
    ).reshape(groups * (window_chunk + entry_chunk), lanes)
    delivered = carry_out(second).reshape(groups, window_chunk + entry_chunk, lanes)
    window_part = delivered[:, :window_chunk].reshape(half_rows, lanes)
    arrived = delivered[:, window_chunk:].reshape(rows_new, lanes)
    window = lax.all_gather(window_part, "tx", axis=0, tiled=True)

    query_cols = query_weight.shape[2]
    heads = query_cols // HEAD_SIZE
    queries = jnp.dot(
        normalized_input,
        query_weight.reshape(width, query_cols),
        preferred_element_type=jnp.float32,
    )
    query_rotated = apply_rotary(
        queries.reshape(rows_new, heads, HEAD_SIZE), token_positions
    ).astype(jnp.bfloat16)
    factor = 1.0 / math.sqrt(HEAD_SIZE)
    rows = jnp.arange(rows_new, dtype=jnp.int32)
    new_mask = rows[None, :] <= rows[:, None]
    cycle = jnp.arange(WINDOW_LENGTH, dtype=jnp.int32)
    held = length - 1 - jnp.mod(offset - 1 - cycle, WINDOW_LENGTH)
    cache_mask = (held[None, :] >= 0) & (held[None, :] > token_positions[:, None] - WINDOW_LENGTH)
    mask_all = jnp.concatenate([cache_mask, new_mask], axis=1)
    keys_all = jnp.concatenate([window[:, :HEAD_SIZE], new_keys], axis=0)
    values_all = jnp.concatenate([window[:, HEAD_SIZE:], new_values], axis=0)

    def one_head(query_rows):
        scores = (
            jnp.einsum("qd,kd->qk", query_rows, keys_all, preferred_element_type=jnp.float32)
            * factor
        )
        scores = jnp.where(mask_all, scores, -jnp.inf)
        top = jnp.max(scores, axis=1, keepdims=True)
        powers = jnp.exp(scores - top)
        total = jnp.sum(powers, axis=1, keepdims=True)
        weights = powers.astype(jnp.bfloat16)
        summed = jnp.dot(weights, values_all, preferred_element_type=jnp.float32)
        return (summed / total).astype(jnp.bfloat16)

    outputs = lax.map(one_head, jnp.transpose(query_rotated, (1, 0, 2)))
    attended = jnp.transpose(outputs, (1, 0, 2)).reshape(rows_new, heads * HEAD_SIZE)

    own_offset = offsets[inverse[request]]
    rolled = jnp.roll(stored, -own_offset, axis=0)
    updated = jnp.roll(jnp.concatenate([arrived, rolled[rows_new:]], axis=0), own_offset, axis=0)
    new_cache = updated[None, None]
    out_rows = output_weight.reshape(output_weight.shape[1], width)
    partial_value = jnp.dot(attended, out_rows, preferred_element_type=jnp.float32)
    across_cores = lax.psum_scatter(
        partial_value.astype(jnp.bfloat16), "tx", scatter_dimension=1, tiled=True
    )
    mixed = lax.psum_scatter(across_cores, "ty", scatter_dimension=1, tiled=True)
    return (mixed, new_cache)


def solution(mesh):
    return jax.shard_map(
        per_device,
        mesh=mesh,
        in_specs=(
            P("dp", "tx"),
            P(None, "ty", "tx"),
            P(None, "ty", None),
            P("ty", "tx", None),
            P("dp", "ty", None, None),
            P(),
            P(),
            P(),
        ),
        out_specs=(P("dp", ("tx", "ty")), P("dp", "ty", None, None)),
        check_vma=False,
    )
```

```python
import math

import jax
import jax.numpy as jnp
from jax import lax
from jax.sharding import PartitionSpec as P

HEAD_SIZE = 64
WINDOW_LENGTH = 2048


EPS = 1e-05


def apply_rotary(values, token_positions):
    width = values.shape[-1]
    half_width = width // 2
    freqs = jnp.exp(jnp.arange(half_width, dtype=jnp.float32) * (-2.0 * math.log(10000.0) / width))
    angles = token_positions.astype(jnp.float32)[:, None] * freqs[None, :]
    cosine = jnp.cos(angles)[:, None, :]
    sine = jnp.sin(angles)[:, None, :]
    leading = values[..., :half_width]
    trailing = values[..., half_width:]
    return jnp.concatenate(
        [leading * cosine - trailing * sine, trailing * cosine + leading * sine], axis=-1
    )


def carry_in(window):
    return lax.all_to_all(window, "dp", split_axis=0, concat_axis=0, tiled=True)


def carry_out(window):
    return lax.all_to_all(window, "dp", split_axis=0, concat_axis=0, tiled=True)


def reorder(window, order, groups):
    columns = window.shape[1]
    blocks = window.reshape(groups, window.shape[0] // groups, columns)
    return jnp.take(blocks, order, axis=0).reshape(window.shape[0], columns)


def per_device(
    tokens, query_weight, key_value_weight, output_weight, cache, lengths, offsets, slots
):
    request = lax.axis_index("dp")
    groups = lax.axis_size("dp")
    halves = lax.axis_size("tx")
    core = lax.axis_index("tx")
    stored = cache[0, 0]
    half_rows = stored.shape[0] // halves
    mine = lax.dynamic_slice_in_dim(stored, core * half_rows, half_rows, axis=0)
    spread = carry_in(mine)
    whole = lax.all_gather(tokens, "tx", axis=1, tiled=True)
    rows_new = whole.shape[0]
    width = whole.shape[1]
    floats = whole.astype(jnp.float32)
    normalized_input = (
        floats * lax.rsqrt(jnp.mean(floats * floats, axis=1, keepdims=True) + EPS)
    ).astype(jnp.bfloat16)
    owners = jnp.arange(slots.shape[0], dtype=jnp.int32)
    inverse = jnp.sum(jnp.where(slots[None, :] == owners[:, None], owners[None, :], 0), axis=1)
    length = lengths[request]
    offset = offsets[request]
    token_positions = length + jnp.arange(rows_new, dtype=jnp.int32)
    rotation_pairs = jnp.dot(
        normalized_input,
        key_value_weight.reshape(width, 2 * HEAD_SIZE),
        preferred_element_type=jnp.float32,
    )
    new_keys = apply_rotary(rotation_pairs[:, None, :HEAD_SIZE], token_positions)[:, 0].astype(
        jnp.bfloat16
    )
    new_values = rotation_pairs[:, HEAD_SIZE:].astype(jnp.bfloat16)
    entry = jnp.concatenate([new_keys, new_values], axis=1)

    window_chunk = half_rows // groups
    entry_chunk = rows_new // groups
    lanes = stored.shape[1]
    second = jnp.concatenate(
        [
            jnp.take(spread.reshape(groups, window_chunk, lanes), slots, axis=0),
            entry.reshape(groups, entry_chunk, lanes),
        ],
        axis=1,
    ).reshape(groups * (window_chunk + entry_chunk), lanes)
    delivered = carry_in(second).reshape(groups, window_chunk + entry_chunk, lanes)
    window_part = delivered[:, :window_chunk].reshape(half_rows, lanes)
    entry_parts = delivered[:, window_chunk:]
    window = lax.all_gather(window_part, "tx", axis=0, tiled=True)

    query_cols = query_weight.shape[2]
    heads = query_cols // HEAD_SIZE
    queries = jnp.dot(
        normalized_input,
        query_weight.reshape(width, query_cols),
        preferred_element_type=jnp.float32,
    )
    query_rotated = apply_rotary(
        queries.reshape(rows_new, heads, HEAD_SIZE), token_positions
    ).astype(jnp.bfloat16)
    factor = 1.0 / math.sqrt(HEAD_SIZE)
    rows = jnp.arange(rows_new, dtype=jnp.int32)
    new_mask = rows[None, :] <= rows[:, None]
    cycle = jnp.arange(WINDOW_LENGTH, dtype=jnp.int32)
    held = length - 1 - jnp.mod(offset - 1 - cycle, WINDOW_LENGTH)
    cache_mask = (held[None, :] >= 0) & (held[None, :] > token_positions[:, None] - WINDOW_LENGTH)
    mask_all = jnp.concatenate([cache_mask, new_mask], axis=1)
    keys_all = jnp.concatenate([window[:, :HEAD_SIZE], new_keys], axis=0)
    values_all = jnp.concatenate([window[:, HEAD_SIZE:], new_values], axis=0)

    def one_head(query_rows):
        scores = (
            jnp.einsum("qd,kd->qk", query_rows, keys_all, preferred_element_type=jnp.float32)
            * factor
        )
        scores = jnp.where(mask_all, scores, -jnp.inf)
        top = jnp.max(scores, axis=1, keepdims=True)
        powers = jnp.exp(scores - top)
        total = jnp.sum(powers, axis=1, keepdims=True)
        weights = powers.astype(jnp.bfloat16)
        summed = jnp.dot(weights, values_all, preferred_element_type=jnp.float32)
        return (summed / total).astype(jnp.bfloat16)

    outputs = lax.map(one_head, jnp.transpose(query_rotated, (1, 0, 2)))
    attended = jnp.transpose(outputs, (1, 0, 2)).reshape(rows_new, heads * HEAD_SIZE)

    arrived = carry_out(jnp.take(entry_parts, inverse, axis=0).reshape(rows_new, lanes))
    own_offset = offsets[inverse[request]]
    rolled = jnp.roll(stored, -own_offset, axis=0)
    updated = jnp.roll(jnp.concatenate([arrived, rolled[rows_new:]], axis=0), own_offset, axis=0)
    new_cache = updated[None, None]
    out_rows = output_weight.reshape(output_weight.shape[1], width)
    partial_value = jnp.dot(attended, out_rows, preferred_element_type=jnp.float32)
    mixed = lax.psum_scatter(
        partial_value.astype(jnp.bfloat16), ("tx", "ty"), scatter_dimension=1, tiled=True
    )
    return (mixed, new_cache)


def solution(mesh):
    return jax.shard_map(
        per_device,
        mesh=mesh,
        in_specs=(
            P("dp", "tx"),
            P(None, "ty", "tx"),
            P(None, "ty", None),
            P("ty", "tx", None),
            P("dp", "ty", None, None),
            P(),
            P(),
            P(),
        ),
        out_specs=(P("dp", ("tx", "ty")), P("dp", "ty", None, None)),
        check_vma=False,
    )
```

```python
import math

import jax
import jax.numpy as jnp
from jax import lax
from jax.sharding import PartitionSpec as P

HEAD_SIZE = 64
WINDOW_LENGTH = 2048


EPS = 1e-05


def apply_rotary(values, token_positions):
    width = values.shape[-1]
    half_width = width // 2
    freqs = jnp.exp(jnp.arange(half_width, dtype=jnp.float32) * (-2.0 * math.log(10000.0) / width))
    angles = token_positions.astype(jnp.float32)[:, None] * freqs[None, :]
    cosine = jnp.cos(angles)[:, None, :]
    sine = jnp.sin(angles)[:, None, :]
    leading = values[..., :half_width]
    trailing = values[..., half_width:]
    return jnp.concatenate(
        [leading * cosine - trailing * sine, trailing * cosine + leading * sine], axis=-1
    )


def carry_in(window):
    return lax.all_to_all(window, "dp", split_axis=0, concat_axis=0, tiled=True)


def carry_out(window):
    return lax.all_to_all(window, "dp", split_axis=0, concat_axis=0, tiled=True)


def reorder(window, order, groups):
    columns = window.shape[1]
    blocks = window.reshape(groups, window.shape[0] // groups, columns)
    return jnp.take(blocks, order, axis=0).reshape(window.shape[0], columns)


def per_device(
    tokens, query_weight, key_value_weight, output_weight, cache, lengths, offsets, slots
):
    request = lax.axis_index("dp")
    groups = lax.axis_size("dp")
    stored = cache[0, 0]
    half_rows = stored.shape[0]
    spread = carry_in(stored)
    whole = lax.all_gather(tokens, "tx", axis=1, tiled=True)
    rows_new = whole.shape[0]
    width = whole.shape[1]
    floats = whole.astype(jnp.float32)
    normalized_input = (
        floats * lax.rsqrt(jnp.mean(floats * floats, axis=1, keepdims=True) + EPS)
    ).astype(jnp.bfloat16)
    owners = jnp.arange(slots.shape[0], dtype=jnp.int32)
    inverse = jnp.sum(jnp.where(slots[None, :] == owners[:, None], owners[None, :], 0), axis=1)
    length = lengths[request]
    offset = offsets[request]
    token_positions = length + jnp.arange(rows_new, dtype=jnp.int32)
    rotation_pairs = jnp.dot(
        normalized_input,
        key_value_weight.reshape(width, 2 * HEAD_SIZE),
        preferred_element_type=jnp.float32,
    )
    new_keys = apply_rotary(rotation_pairs[:, None, :HEAD_SIZE], token_positions)[:, 0].astype(
        jnp.bfloat16
    )
    new_values = rotation_pairs[:, HEAD_SIZE:].astype(jnp.bfloat16)
    entry = jnp.concatenate([new_keys, new_values], axis=1)

    window_chunk = half_rows // groups
    entry_chunk = rows_new // groups
    lanes = stored.shape[1]
    second = jnp.concatenate(
        [
            jnp.take(spread.reshape(groups, window_chunk, lanes), slots, axis=0),
            entry.reshape(groups, entry_chunk, lanes),
        ],
        axis=1,
    ).reshape(groups * (window_chunk + entry_chunk), lanes)
    delivered = carry_in(second).reshape(groups, window_chunk + entry_chunk, lanes)
    window = delivered[:, :window_chunk].reshape(half_rows, lanes)
    entry_parts = delivered[:, window_chunk:]

    query_cols = query_weight.shape[2]
    heads = query_cols // HEAD_SIZE
    queries = jnp.dot(
        normalized_input,
        query_weight.reshape(width, query_cols),
        preferred_element_type=jnp.float32,
    )
    query_rotated = apply_rotary(
        queries.reshape(rows_new, heads, HEAD_SIZE), token_positions
    ).astype(jnp.bfloat16)
    factor = 1.0 / math.sqrt(HEAD_SIZE)
    rows = jnp.arange(rows_new, dtype=jnp.int32)
    new_mask = rows[None, :] <= rows[:, None]
    cycle = jnp.arange(WINDOW_LENGTH, dtype=jnp.int32)
    held = length - 1 - jnp.mod(offset - 1 - cycle, WINDOW_LENGTH)
    cache_mask = (held[None, :] >= 0) & (held[None, :] > token_positions[:, None] - WINDOW_LENGTH)
    mask_all = jnp.concatenate([cache_mask, new_mask], axis=1)
    keys_all = jnp.concatenate([window[:, :HEAD_SIZE], new_keys], axis=0)
    values_all = jnp.concatenate([window[:, HEAD_SIZE:], new_values], axis=0)

    def one_head(query_rows):
        scores = (
            jnp.einsum("qd,kd->qk", query_rows, keys_all, preferred_element_type=jnp.float32)
            * factor
        )
        scores = jnp.where(mask_all, scores, -jnp.inf)
        top = jnp.max(scores, axis=1, keepdims=True)
        powers = jnp.exp(scores - top)
        total = jnp.sum(powers, axis=1, keepdims=True)
        weights = powers.astype(jnp.bfloat16)
        summed = jnp.dot(weights, values_all, preferred_element_type=jnp.float32)
        return (summed / total).astype(jnp.bfloat16)

    outputs = lax.map(one_head, jnp.transpose(query_rotated, (1, 0, 2)))
    attended = jnp.transpose(outputs, (1, 0, 2)).reshape(rows_new, heads * HEAD_SIZE)

    arrived = carry_out(jnp.take(entry_parts, inverse, axis=0).reshape(rows_new, lanes))
    own_offset = offsets[inverse[request]]
    rolled = jnp.roll(stored, -own_offset, axis=0)
    updated = jnp.roll(jnp.concatenate([arrived, rolled[rows_new:]], axis=0), own_offset, axis=0)
    new_cache = updated[None, None]
    out_rows = output_weight.reshape(output_weight.shape[1], width)
    partial_value = jnp.dot(attended, out_rows, preferred_element_type=jnp.float32)
    mixed = lax.psum_scatter(
        partial_value.astype(jnp.bfloat16), ("tx", "ty"), scatter_dimension=1, tiled=True
    )
    return (mixed, new_cache)


def solution(mesh):
    return jax.shard_map(
        per_device,
        mesh=mesh,
        in_specs=(
            P("dp", "tx"),
            P(None, "ty", "tx"),
            P(None, "ty", None),
            P("ty", "tx", None),
            P("dp", "ty", None, None),
            P(),
            P(),
            P(),
        ),
        out_specs=(P("dp", ("tx", "ty")), P("dp", "ty", None, None)),
        check_vma=False,
    )
```

```python
import math

import jax
import jax.numpy as jnp
from jax import lax
from jax.experimental import pallas as pl
from jax.sharding import PartitionSpec as P

HEAD_SIZE = 64
WINDOW_LENGTH = 2048


EPS = 1e-05


def apply_rotary(values, token_positions):
    width = values.shape[-1]
    half_width = width // 2
    freqs = jnp.exp(jnp.arange(half_width, dtype=jnp.float32) * (-2.0 * math.log(10000.0) / width))
    angles = token_positions.astype(jnp.float32)[:, None] * freqs[None, :]
    cosine = jnp.cos(angles)[:, None, :]
    sine = jnp.sin(angles)[:, None, :]
    leading = values[..., :half_width]
    trailing = values[..., half_width:]
    return jnp.concatenate(
        [leading * cosine - trailing * sine, trailing * cosine + leading * sine], axis=-1
    )


def attention_kernel(q_ref, win_ref, ent_ref, lim_ref, age_ref, o_ref):
    rows = q_ref.shape[1]
    block = pl.program_id(0)
    factor = 1.0 / math.sqrt(HEAD_SIZE)
    q = q_ref[0]
    win = win_ref[...]
    ent = ent_ref[...]
    dims = (((1,), (1,)), ((), ()))
    s_old = lax.dot_general(q, win, dims, preferred_element_type=jnp.float32) * factor
    s_new = lax.dot_general(q, ent, dims, preferred_element_type=jnp.float32) * factor
    s_old = jnp.where(age_ref[...] < lim_ref[...], s_old, -jnp.inf)
    row_ids = block * rows + lax.broadcasted_iota(jnp.int32, s_new.shape, 0)
    col_ids = lax.broadcasted_iota(jnp.int32, s_new.shape, 1)
    s_new = jnp.where(col_ids <= row_ids, s_new, -jnp.inf)
    top = jnp.maximum(jnp.max(s_old, axis=1, keepdims=True), jnp.max(s_new, axis=1, keepdims=True))
    p_old = jnp.exp(s_old - top)
    p_new = jnp.exp(s_new - top)
    total = jnp.sum(p_old, axis=1, keepdims=True) + jnp.sum(p_new, axis=1, keepdims=True)
    acc = jnp.dot(p_old.astype(jnp.bfloat16), win, preferred_element_type=jnp.float32)
    acc = acc + jnp.dot(p_new.astype(jnp.bfloat16), ent, preferred_element_type=jnp.float32)
    o_ref[0] = (acc / total).astype(o_ref.dtype)


def attend(query_rotated, window, entry, length, offset):
    rows_new, heads, _ = query_rotated.shape
    lanes = window.shape[1]
    padded = jnp.concatenate(
        [jnp.transpose(query_rotated, (1, 0, 2)),
         jnp.zeros((heads, rows_new, lanes - HEAD_SIZE), query_rotated.dtype)], axis=2)
    rows = jnp.arange(rows_new, dtype=jnp.int32)
    limit = jnp.minimum(length, WINDOW_LENGTH - 1 - rows)[:, None]
    cycle = jnp.arange(window.shape[0], dtype=jnp.int32)
    age = jnp.mod(offset - 1 - cycle, WINDOW_LENGTH)[None, :]
    block = 128
    out = pl.pallas_call(
        attention_kernel,
        grid=(rows_new // block, heads),
        in_specs=[
            pl.BlockSpec((1, block, lanes), lambda b, h: (h, b, 0)),
            pl.BlockSpec(window.shape, lambda b, h: (0, 0)),
            pl.BlockSpec(entry.shape, lambda b, h: (0, 0)),
            pl.BlockSpec((block, 1), lambda b, h: (b, 0)),
            pl.BlockSpec((1, window.shape[0]), lambda b, h: (0, 0)),
        ],
        out_specs=pl.BlockSpec((1, block, lanes), lambda b, h: (h, b, 0)),
        out_shape=jax.ShapeDtypeStruct((heads, rows_new, lanes), jnp.bfloat16),
    )(padded, window, entry, limit, age)
    return jnp.transpose(out[:, :, HEAD_SIZE:], (1, 0, 2)).reshape(rows_new, heads * HEAD_SIZE)


def carry_in(window):
    return lax.all_to_all(window, "dp", split_axis=0, concat_axis=0, tiled=True)


def carry_out(window):
    return lax.all_to_all(window, "dp", split_axis=0, concat_axis=0, tiled=True)


def reorder(window, order, groups):
    columns = window.shape[1]
    blocks = window.reshape(groups, window.shape[0] // groups, columns)
    return jnp.take(blocks, order, axis=0).reshape(window.shape[0], columns)


def per_device(
    tokens, query_weight, key_value_weight, output_weight, cache, lengths, offsets, slots
):
    request = lax.axis_index("dp")
    groups = lax.axis_size("dp")
    stored = cache[0, 0]
    half_rows = stored.shape[0]
    spread = carry_in(stored)
    whole = lax.all_gather(tokens, "tx", axis=1, tiled=True)
    rows_new = whole.shape[0]
    width = whole.shape[1]
    floats = whole.astype(jnp.float32)
    normalized_input = (
        floats * lax.rsqrt(jnp.mean(floats * floats, axis=1, keepdims=True) + EPS)
    ).astype(jnp.bfloat16)
    owners = jnp.arange(slots.shape[0], dtype=jnp.int32)
    inverse = jnp.sum(jnp.where(slots[None, :] == owners[:, None], owners[None, :], 0), axis=1)
    length = lengths[request]
    offset = offsets[request]
    token_positions = length + jnp.arange(rows_new, dtype=jnp.int32)
    rotation_pairs = jnp.dot(
        normalized_input,
        key_value_weight.reshape(width, 2 * HEAD_SIZE),
        preferred_element_type=jnp.float32,
    )
    new_keys = apply_rotary(rotation_pairs[:, None, :HEAD_SIZE], token_positions)[:, 0].astype(
        jnp.bfloat16
    )
    new_values = rotation_pairs[:, HEAD_SIZE:].astype(jnp.bfloat16)
    entry = jnp.concatenate([new_keys, new_values], axis=1)

    window_chunk = half_rows // groups
    entry_chunk = rows_new // groups
    lanes = stored.shape[1]
    second = jnp.concatenate(
        [
            jnp.take(spread.reshape(groups, window_chunk, lanes), slots, axis=0),
            entry.reshape(groups, entry_chunk, lanes),
        ],
        axis=1,
    ).reshape(groups * (window_chunk + entry_chunk), lanes)
    delivered = carry_in(second).reshape(groups, window_chunk + entry_chunk, lanes)
    window = delivered[:, :window_chunk].reshape(half_rows, lanes)
    entry_parts = delivered[:, window_chunk:]

    query_cols = query_weight.shape[2]
    heads = query_cols // HEAD_SIZE
    queries = jnp.dot(
        normalized_input,
        query_weight.reshape(width, query_cols),
        preferred_element_type=jnp.float32,
    )
    query_rotated = apply_rotary(
        queries.reshape(rows_new, heads, HEAD_SIZE), token_positions
    ).astype(jnp.bfloat16)
    attended = attend(query_rotated, window, entry, length, offset)

    arrived = carry_out(jnp.take(entry_parts, inverse, axis=0).reshape(rows_new, lanes))
    own_offset = offsets[inverse[request]]
    rolled = jnp.roll(stored, -own_offset, axis=0)
    updated = jnp.roll(jnp.concatenate([arrived, rolled[rows_new:]], axis=0), own_offset, axis=0)
    new_cache = updated[None, None]
    out_rows = output_weight.reshape(output_weight.shape[1], width)
    partial_value = jnp.dot(attended, out_rows, preferred_element_type=jnp.float32)
    mixed = lax.psum_scatter(
        partial_value.astype(jnp.bfloat16), ("tx", "ty"), scatter_dimension=1, tiled=True
    )
    return (mixed, new_cache)


def solution(mesh):
    return jax.shard_map(
        per_device,
        mesh=mesh,
        in_specs=(
            P("dp", "tx"),
            P(None, "ty", "tx"),
            P(None, "ty", None),
            P("ty", "tx", None),
            P("dp", "ty", None, None),
            P(),
            P(),
            P(),
        ),
        out_specs=(P("dp", ("tx", "ty")), P("dp", "ty", None, None)),
        check_vma=False,
    )
```

```python
import math

import jax
import jax.numpy as jnp
from jax import lax
from jax.experimental import pallas as pl
from jax.sharding import PartitionSpec as P

HEAD_SIZE = 64
WINDOW_LENGTH = 2048


EPS = 1e-05


def apply_rotary(values, token_positions):
    width = values.shape[-1]
    half_width = width // 2
    freqs = jnp.exp(jnp.arange(half_width, dtype=jnp.float32) * (-2.0 * math.log(10000.0) / width))
    angles = token_positions.astype(jnp.float32)[:, None] * freqs[None, :]
    cosine = jnp.cos(angles)[:, None, :]
    sine = jnp.sin(angles)[:, None, :]
    leading = values[..., :half_width]
    trailing = values[..., half_width:]
    return jnp.concatenate(
        [leading * cosine - trailing * sine, trailing * cosine + leading * sine], axis=-1
    )


def attention_kernel(q_ref, win_ref, ent_ref, win_t_ref, ent_t_ref, lim_ref, age_ref, o_ref):
    rows = q_ref.shape[1]
    block = pl.program_id(0)
    q = q_ref[0]
    win = win_ref[...]
    ent = ent_ref[...]
    s_old = jnp.dot(q, win_t_ref[...], preferred_element_type=jnp.float32)
    s_new = jnp.dot(q, ent_t_ref[...], preferred_element_type=jnp.float32)
    s_old = jnp.where(age_ref[...] < lim_ref[...], s_old, -jnp.inf)
    row_ids = block * rows + lax.broadcasted_iota(jnp.int32, s_new.shape, 0)
    col_ids = lax.broadcasted_iota(jnp.int32, s_new.shape, 1)
    s_new = jnp.where(col_ids <= row_ids, s_new, -jnp.inf)
    top = jnp.maximum(jnp.max(s_old, axis=1, keepdims=True), jnp.max(s_new, axis=1, keepdims=True))
    p_old = jnp.exp(s_old - top)
    p_new = jnp.exp(s_new - top)
    total = jnp.sum(p_old, axis=1, keepdims=True) + jnp.sum(p_new, axis=1, keepdims=True)
    acc = jnp.dot(p_old.astype(jnp.bfloat16), win, preferred_element_type=jnp.float32)
    acc = acc + jnp.dot(p_new.astype(jnp.bfloat16), ent, preferred_element_type=jnp.float32)
    o_ref[0] = (acc / total).astype(o_ref.dtype)


def attend(query_rotated, window, entry, length, offset):
    rows_new, heads, _ = query_rotated.shape
    lanes = window.shape[1]
    factor = 1.0 / math.sqrt(HEAD_SIZE)
    scaled = query_rotated * jnp.asarray(factor, query_rotated.dtype)
    padded = jnp.concatenate(
        [jnp.transpose(scaled, (1, 0, 2)),
         jnp.zeros((heads, rows_new, lanes - HEAD_SIZE), query_rotated.dtype)], axis=2)
    rows = jnp.arange(rows_new, dtype=jnp.int32)
    limit = jnp.minimum(length, WINDOW_LENGTH - 1 - rows)[:, None]
    cycle = jnp.arange(window.shape[0], dtype=jnp.int32)
    age = jnp.mod(offset - 1 - cycle, WINDOW_LENGTH)[None, :]
    block = 128
    out = pl.pallas_call(
        attention_kernel,
        grid=(rows_new // block, heads),
        in_specs=[
            pl.BlockSpec((1, block, lanes), lambda b, h: (h, b, 0)),
            pl.BlockSpec(window.shape, lambda b, h: (0, 0)),
            pl.BlockSpec(entry.shape, lambda b, h: (0, 0)),
            pl.BlockSpec((lanes, window.shape[0]), lambda b, h: (0, 0)),
            pl.BlockSpec((lanes, entry.shape[0]), lambda b, h: (0, 0)),
            pl.BlockSpec((block, 1), lambda b, h: (b, 0)),
            pl.BlockSpec((1, window.shape[0]), lambda b, h: (0, 0)),
        ],
        out_specs=pl.BlockSpec((1, block, lanes), lambda b, h: (h, b, 0)),
        out_shape=jax.ShapeDtypeStruct((heads, rows_new, lanes), jnp.bfloat16),
    )(padded, window, entry, window.T, entry.T, limit, age)
    return jnp.transpose(out[:, :, HEAD_SIZE:], (1, 0, 2)).reshape(rows_new, heads * HEAD_SIZE)


def carry_in(window):
    return lax.all_to_all(window, "dp", split_axis=0, concat_axis=0, tiled=True)


def carry_out(window):
    return lax.all_to_all(window, "dp", split_axis=0, concat_axis=0, tiled=True)


def reorder(window, order, groups):
    columns = window.shape[1]
    blocks = window.reshape(groups, window.shape[0] // groups, columns)
    return jnp.take(blocks, order, axis=0).reshape(window.shape[0], columns)


def per_device(
    tokens, query_weight, key_value_weight, output_weight, cache, lengths, offsets, slots
):
    request = lax.axis_index("dp")
    groups = lax.axis_size("dp")
    stored = cache[0, 0]
    half_rows = stored.shape[0]
    spread = carry_in(stored)
    whole = lax.all_gather(tokens, "tx", axis=1, tiled=True)
    rows_new = whole.shape[0]
    width = whole.shape[1]
    floats = whole.astype(jnp.float32)
    normalized_input = (
        floats * lax.rsqrt(jnp.mean(floats * floats, axis=1, keepdims=True) + EPS)
    ).astype(jnp.bfloat16)
    owners = jnp.arange(slots.shape[0], dtype=jnp.int32)
    inverse = jnp.sum(jnp.where(slots[None, :] == owners[:, None], owners[None, :], 0), axis=1)
    length = lengths[request]
    offset = offsets[request]
    token_positions = length + jnp.arange(rows_new, dtype=jnp.int32)
    rotation_pairs = jnp.dot(
        normalized_input,
        key_value_weight.reshape(width, 2 * HEAD_SIZE),
        preferred_element_type=jnp.float32,
    )
    new_keys = apply_rotary(rotation_pairs[:, None, :HEAD_SIZE], token_positions)[:, 0].astype(
        jnp.bfloat16
    )
    new_values = rotation_pairs[:, HEAD_SIZE:].astype(jnp.bfloat16)
    entry = jnp.concatenate([new_keys, new_values], axis=1)

    window_chunk = half_rows // groups
    entry_chunk = rows_new // groups
    lanes = stored.shape[1]
    second = jnp.concatenate(
        [
            jnp.take(spread.reshape(groups, window_chunk, lanes), slots, axis=0),
            entry.reshape(groups, entry_chunk, lanes),
        ],
        axis=1,
    ).reshape(groups * (window_chunk + entry_chunk), lanes)
    delivered = carry_in(second).reshape(groups, window_chunk + entry_chunk, lanes)
    window = delivered[:, :window_chunk].reshape(half_rows, lanes)
    entry_parts = delivered[:, window_chunk:]

    query_cols = query_weight.shape[2]
    heads = query_cols // HEAD_SIZE
    queries = jnp.dot(
        normalized_input,
        query_weight.reshape(width, query_cols),
        preferred_element_type=jnp.float32,
    )
    query_rotated = apply_rotary(
        queries.reshape(rows_new, heads, HEAD_SIZE), token_positions
    ).astype(jnp.bfloat16)
    attended = attend(query_rotated, window, entry, length, offset)

    arrived = carry_out(jnp.take(entry_parts, inverse, axis=0).reshape(rows_new, lanes))
    own_offset = offsets[inverse[request]]
    rolled = jnp.roll(stored, -own_offset, axis=0)
    updated = jnp.roll(jnp.concatenate([arrived, rolled[rows_new:]], axis=0), own_offset, axis=0)
    new_cache = updated[None, None]
    out_rows = output_weight.reshape(output_weight.shape[1], width)
    partial_value = jnp.dot(attended, out_rows, preferred_element_type=jnp.float32)
    mixed = lax.psum_scatter(
        partial_value.astype(jnp.bfloat16), ("tx", "ty"), scatter_dimension=1, tiled=True
    )
    return (mixed, new_cache)


def solution(mesh):
    return jax.shard_map(
        per_device,
        mesh=mesh,
        in_specs=(
            P("dp", "tx"),
            P(None, "ty", "tx"),
            P(None, "ty", None),
            P("ty", "tx", None),
            P("dp", "ty", None, None),
            P(),
            P(),
            P(),
        ),
        out_specs=(P("dp", ("tx", "ty")), P("dp", "ty", None, None)),
        check_vma=False,
    )
```

```python
import math

import jax
import jax.numpy as jnp
from jax import lax
from jax.sharding import PartitionSpec as P

HEAD_SIZE = 64
WINDOW_LENGTH = 2048


EPS = 1e-05


def apply_rotary(values, token_positions):
    width = values.shape[-1]
    half_width = width // 2
    freqs = jnp.exp(jnp.arange(half_width, dtype=jnp.float32) * (-2.0 * math.log(10000.0) / width))
    angles = token_positions.astype(jnp.float32)[:, None] * freqs[None, :]
    cosine = jnp.cos(angles)[:, None, :]
    sine = jnp.sin(angles)[:, None, :]
    leading = values[..., :half_width]
    trailing = values[..., half_width:]
    return jnp.concatenate(
        [leading * cosine - trailing * sine, trailing * cosine + leading * sine], axis=-1
    )


def carry_in(window):
    return lax.all_to_all(window, "dp", split_axis=0, concat_axis=0, tiled=True)


def carry_out(window):
    return lax.all_to_all(window, "dp", split_axis=0, concat_axis=0, tiled=True)


def reorder(window, order, groups):
    columns = window.shape[1]
    blocks = window.reshape(groups, window.shape[0] // groups, columns)
    return jnp.take(blocks, order, axis=0).reshape(window.shape[0], columns)


def per_device(
    tokens, query_weight, key_value_weight, output_weight, cache, lengths, offsets, slots
):
    request = lax.axis_index("dp")
    groups = lax.axis_size("dp")
    stored = cache[0, 0]
    half_rows = stored.shape[0]
    spread = carry_in(stored)
    whole = lax.all_gather(tokens, "tx", axis=1, tiled=True)
    rows_new = whole.shape[0]
    width = whole.shape[1]
    floats = whole.astype(jnp.float32)
    normalized_input = (
        floats * lax.rsqrt(jnp.mean(floats * floats, axis=1, keepdims=True) + EPS)
    ).astype(jnp.bfloat16)
    owners = jnp.arange(slots.shape[0], dtype=jnp.int32)
    inverse = jnp.sum(jnp.where(slots[None, :] == owners[:, None], owners[None, :], 0), axis=1)
    length = lengths[request]
    offset = offsets[request]
    token_positions = length + jnp.arange(rows_new, dtype=jnp.int32)
    rotation_pairs = jnp.dot(
        normalized_input,
        key_value_weight.reshape(width, 2 * HEAD_SIZE),
        preferred_element_type=jnp.float32,
    )
    new_keys = apply_rotary(rotation_pairs[:, None, :HEAD_SIZE], token_positions)[:, 0].astype(
        jnp.bfloat16
    )
    new_values = rotation_pairs[:, HEAD_SIZE:].astype(jnp.bfloat16)
    entry = jnp.concatenate([new_keys, new_values], axis=1)

    window_chunk = half_rows // groups
    entry_chunk = rows_new // groups
    lanes = stored.shape[1]
    second = jnp.concatenate(
        [
            jnp.take(spread.reshape(groups, window_chunk, lanes), slots, axis=0),
            entry.reshape(groups, entry_chunk, lanes),
        ],
        axis=1,
    ).reshape(groups * (window_chunk + entry_chunk), lanes)
    delivered = carry_in(second).reshape(groups, window_chunk + entry_chunk, lanes)
    window = delivered[:, :window_chunk].reshape(half_rows, lanes)
    entry_parts = delivered[:, window_chunk:]

    query_cols = query_weight.shape[2]
    heads = query_cols // HEAD_SIZE
    queries = jnp.dot(
        normalized_input,
        query_weight.reshape(width, query_cols),
        preferred_element_type=jnp.float32,
    )
    query_rotated = apply_rotary(
        queries.reshape(rows_new, heads, HEAD_SIZE), token_positions
    ).astype(jnp.bfloat16)
    factor = 1.0 / math.sqrt(HEAD_SIZE)
    rows = jnp.arange(rows_new, dtype=jnp.int32)
    new_mask = rows[None, :] <= rows[:, None]
    cycle = jnp.arange(WINDOW_LENGTH, dtype=jnp.int32)
    held = length - 1 - jnp.mod(offset - 1 - cycle, WINDOW_LENGTH)
    cache_mask = (held[None, :] >= 0) & (held[None, :] > token_positions[:, None] - WINDOW_LENGTH)
    mask_all = jnp.concatenate([cache_mask, new_mask], axis=1)
    keys_all = jnp.concatenate([window[:, :HEAD_SIZE], new_keys], axis=0)
    values_all = jnp.concatenate([window[:, HEAD_SIZE:], new_values], axis=0)

    def one_head(query_rows):
        scores = (
            jnp.einsum("qd,kd->qk", query_rows, keys_all, preferred_element_type=jnp.float32)
            * factor
        )
        scores = jnp.where(mask_all, scores, -jnp.inf)
        top = jnp.max(scores, axis=1, keepdims=True)
        powers = jnp.exp(scores - top)
        total = jnp.sum(powers, axis=1, keepdims=True)
        weights = powers.astype(jnp.bfloat16)
        summed = jnp.dot(weights, values_all, preferred_element_type=jnp.float32)
        return (summed / total).astype(jnp.bfloat16)

    outputs = lax.map(one_head, jnp.transpose(query_rotated, (1, 0, 2)))
    attended = jnp.transpose(outputs, (1, 0, 2)).reshape(rows_new, heads * HEAD_SIZE)

    arrived = carry_out(jnp.take(entry_parts, inverse, axis=0).reshape(rows_new, lanes))
    own_offset = offsets[inverse[request]]
    rolled = jnp.roll(stored, -own_offset, axis=0)
    updated = jnp.roll(jnp.concatenate([arrived, rolled[rows_new:]], axis=0), own_offset, axis=0)
    new_cache = updated[None, None]
    out_rows = output_weight.reshape(output_weight.shape[1], width)
    partial_value = jnp.dot(attended, out_rows, preferred_element_type=jnp.float32)
    halves = lax.axis_size("tx")
    if halves == 2:
        core = lax.axis_index("tx")
        half_cols = width // halves
        kept = lax.dynamic_slice_in_dim(partial_value, core * half_cols, half_cols, axis=1)
        sent = lax.dynamic_slice_in_dim(partial_value, (1 - core) * half_cols, half_cols, axis=1)
        across_cores = kept + lax.ppermute(sent, "tx", [(0, 1), (1, 0)])
    else:
        across_cores = lax.psum_scatter(partial_value, "tx", scatter_dimension=1, tiled=True)
    mixed = lax.psum_scatter(
        across_cores.astype(jnp.bfloat16), "ty", scatter_dimension=1, tiled=True
    )
    return (mixed, new_cache)


def solution(mesh):
    return jax.shard_map(
        per_device,
        mesh=mesh,
        in_specs=(
            P("dp", "tx"),
            P(None, "ty", "tx"),
            P(None, "ty", None),
            P("ty", "tx", None),
            P("dp", "ty", None, None),
            P(),
            P(),
            P(),
        ),
        out_specs=(P("dp", ("tx", "ty")), P("dp", "ty", None, None)),
        check_vma=False,
    )
```

```python
import math

import jax
import jax.numpy as jnp
from jax import lax
from jax.sharding import PartitionSpec as P

HEAD_SIZE = 64
WINDOW_LENGTH = 2048


EPS = 1e-05


def apply_rotary(values, token_positions):
    width = values.shape[-1]
    half_width = width // 2
    freqs = jnp.exp(jnp.arange(half_width, dtype=jnp.float32) * (-2.0 * math.log(10000.0) / width))
    angles = token_positions.astype(jnp.float32)[:, None] * freqs[None, :]
    cosine = jnp.cos(angles)[:, None, :]
    sine = jnp.sin(angles)[:, None, :]
    leading = values[..., :half_width]
    trailing = values[..., half_width:]
    return jnp.concatenate(
        [leading * cosine - trailing * sine, trailing * cosine + leading * sine], axis=-1
    )


def carry_in(window):
    return lax.all_to_all(window, "dp", split_axis=0, concat_axis=0, tiled=True)


def carry_out(window):
    return lax.all_to_all(window, "dp", split_axis=0, concat_axis=0, tiled=True)


def reorder(window, order, groups):
    columns = window.shape[1]
    blocks = window.reshape(groups, window.shape[0] // groups, columns)
    return jnp.take(blocks, order, axis=0).reshape(window.shape[0], columns)


def per_device(
    tokens, query_weight, key_value_weight, output_weight, cache, lengths, offsets, slots
):
    request = lax.axis_index("dp")
    groups = lax.axis_size("dp")
    stored = cache[0, 0]
    half_rows = stored.shape[0]
    spread = carry_in(stored)
    whole = lax.all_gather(tokens, "tx", axis=1, tiled=True)
    rows_new = whole.shape[0]
    width = whole.shape[1]
    floats = whole.astype(jnp.float32)
    normalized_input = (
        floats * lax.rsqrt(jnp.mean(floats * floats, axis=1, keepdims=True) + EPS)
    ).astype(jnp.bfloat16)
    owners = jnp.arange(slots.shape[0], dtype=jnp.int32)
    inverse = jnp.sum(jnp.where(slots[None, :] == owners[:, None], owners[None, :], 0), axis=1)
    length = lengths[request]
    offset = offsets[request]
    token_positions = length + jnp.arange(rows_new, dtype=jnp.int32)
    rotation_pairs = jnp.dot(
        normalized_input,
        key_value_weight.reshape(width, 2 * HEAD_SIZE),
        preferred_element_type=jnp.float32,
    )
    new_keys = apply_rotary(rotation_pairs[:, None, :HEAD_SIZE], token_positions)[:, 0].astype(
        jnp.bfloat16
    )
    new_values = rotation_pairs[:, HEAD_SIZE:].astype(jnp.bfloat16)
    entry = jnp.concatenate([new_keys, new_values], axis=1)

    window_chunk = half_rows // groups
    entry_chunk = rows_new // groups
    lanes = stored.shape[1]
    second = jnp.concatenate(
        [
            jnp.take(spread.reshape(groups, window_chunk, lanes), slots, axis=0),
            entry.reshape(groups, entry_chunk, lanes),
        ],
        axis=1,
    ).reshape(groups * (window_chunk + entry_chunk), lanes)
    delivered = carry_in(second).reshape(groups, window_chunk + entry_chunk, lanes)
    window = delivered[:, :window_chunk].reshape(half_rows, lanes)
    entry_parts = delivered[:, window_chunk:]

    query_cols = query_weight.shape[2]
    heads = query_cols // HEAD_SIZE
    queries = jnp.dot(
        normalized_input,
        query_weight.reshape(width, query_cols),
        preferred_element_type=jnp.float32,
    )
    query_rotated = apply_rotary(
        queries.reshape(rows_new, heads, HEAD_SIZE), token_positions
    ).astype(jnp.bfloat16)
    factor = 1.0 / math.sqrt(HEAD_SIZE)
    rows = jnp.arange(rows_new, dtype=jnp.int32)
    new_mask = rows[None, :] <= rows[:, None]
    cycle = jnp.arange(WINDOW_LENGTH, dtype=jnp.int32)
    held = length - 1 - jnp.mod(offset - 1 - cycle, WINDOW_LENGTH)
    cache_mask = (held[None, :] >= 0) & (held[None, :] > token_positions[:, None] - WINDOW_LENGTH)
    mask_all = jnp.concatenate([cache_mask, new_mask], axis=1)
    keys_all = jnp.concatenate([window[:, :HEAD_SIZE], new_keys], axis=0)
    values_all = jnp.concatenate([window[:, HEAD_SIZE:], new_values], axis=0)

    def one_head(query_rows):
        scores = (
            jnp.einsum("qd,kd->qk", query_rows, keys_all, preferred_element_type=jnp.float32)
            * factor
        )
        scores = jnp.where(mask_all, scores, -jnp.inf)
        top = jnp.max(scores, axis=1, keepdims=True)
        powers = jnp.exp(scores - top)
        total = jnp.sum(powers, axis=1, keepdims=True)
        weights = powers.astype(jnp.bfloat16)
        summed = jnp.dot(weights, values_all, preferred_element_type=jnp.float32)
        return (summed / total).astype(jnp.bfloat16)

    outputs = lax.map(one_head, jnp.transpose(query_rotated, (1, 0, 2)))
    attended = jnp.transpose(outputs, (1, 0, 2)).reshape(rows_new, heads * HEAD_SIZE)

    arrived = carry_out(jnp.take(entry_parts, inverse, axis=0).reshape(rows_new, lanes))
    own_offset = offsets[inverse[request]]
    extended = jnp.concatenate([stored, stored[:rows_new]], axis=0)
    extended = lax.dynamic_update_slice_in_dim(extended, arrived, own_offset, axis=0)
    wrap = own_offset + rows_new - WINDOW_LENGTH
    head_rows = jnp.arange(rows_new, dtype=jnp.int32)[:, None]
    head = jnp.where(head_rows < wrap, extended[WINDOW_LENGTH:], extended[:rows_new])
    updated = jnp.concatenate([head, extended[rows_new:WINDOW_LENGTH]], axis=0)
    new_cache = updated[None, None]
    out_rows = output_weight.reshape(output_weight.shape[1], width)
    halves = lax.axis_size("tx")
    if halves == 2:
        core = lax.axis_index("tx")
        half_cols = width // halves
        sent = jnp.dot(
            attended,
            lax.dynamic_slice_in_dim(out_rows, (1 - core) * half_cols, half_cols, axis=1),
            preferred_element_type=jnp.float32,
        )
        received = lax.ppermute(sent, "tx", [(0, 1), (1, 0)])
        kept = jnp.dot(
            attended,
            lax.dynamic_slice_in_dim(out_rows, core * half_cols, half_cols, axis=1),
            preferred_element_type=jnp.float32,
        )
        across_cores = kept + received
    else:
        partial_value = jnp.dot(attended, out_rows, preferred_element_type=jnp.float32)
        across_cores = lax.psum_scatter(partial_value, "tx", scatter_dimension=1, tiled=True)
    mixed = lax.psum_scatter(
        across_cores.astype(jnp.bfloat16), "ty", scatter_dimension=1, tiled=True
    )
    return (mixed, new_cache)


def solution(mesh):
    return jax.shard_map(
        per_device,
        mesh=mesh,
        in_specs=(
            P("dp", "tx"),
            P(None, "ty", "tx"),
            P(None, "ty", None),
            P("ty", "tx", None),
            P("dp", "ty", None, None),
            P(),
            P(),
            P(),
        ),
        out_specs=(P("dp", ("tx", "ty")), P("dp", "ty", None, None)),
        check_vma=False,
    )
```

```python
import math

import jax
import jax.numpy as jnp
from jax import lax
from jax.sharding import PartitionSpec as P

HEAD_SIZE = 64
WINDOW_LENGTH = 2048


EPS = 1e-05


def apply_rotary(values, token_positions):
    width = values.shape[-1]
    half_width = width // 2
    freqs = jnp.exp(jnp.arange(half_width, dtype=jnp.float32) * (-2.0 * math.log(10000.0) / width))
    angles = token_positions.astype(jnp.float32)[:, None] * freqs[None, :]
    cosine = jnp.cos(angles)[:, None, :]
    sine = jnp.sin(angles)[:, None, :]
    leading = values[..., :half_width]
    trailing = values[..., half_width:]
    return jnp.concatenate(
        [leading * cosine - trailing * sine, trailing * cosine + leading * sine], axis=-1
    )


def carry_in(window):
    return lax.all_to_all(window, "dp", split_axis=0, concat_axis=0, tiled=True)


def carry_out(window):
    return lax.all_to_all(window, "dp", split_axis=0, concat_axis=0, tiled=True)


def reorder(window, order, groups):
    columns = window.shape[1]
    blocks = window.reshape(groups, window.shape[0] // groups, columns)
    return jnp.take(blocks, order, axis=0).reshape(window.shape[0], columns)


def per_device(
    tokens, query_weight, key_value_weight, output_weight, cache, lengths, offsets, slots
):
    request = lax.axis_index("dp")
    groups = lax.axis_size("dp")
    stored = cache[0, 0]
    half_rows = stored.shape[0]
    spread = carry_in(stored)
    if lax.axis_size("tx") == 2:
        core = lax.axis_index("tx")
        other = lax.ppermute(tokens, "tx", [(0, 1), (1, 0)])
        whole = jnp.where(
            core == 0,
            jnp.concatenate([tokens, other], axis=1),
            jnp.concatenate([other, tokens], axis=1),
        )
    else:
        whole = lax.all_gather(tokens, "tx", axis=1, tiled=True)
    rows_new = whole.shape[0]
    width = whole.shape[1]
    floats = whole.astype(jnp.float32)
    normalized_input = (
        floats * lax.rsqrt(jnp.mean(floats * floats, axis=1, keepdims=True) + EPS)
    ).astype(jnp.bfloat16)
    owners = jnp.arange(slots.shape[0], dtype=jnp.int32)
    inverse = jnp.sum(jnp.where(slots[None, :] == owners[:, None], owners[None, :], 0), axis=1)
    length = lengths[request]
    offset = offsets[request]
    token_positions = length + jnp.arange(rows_new, dtype=jnp.int32)
    rotation_pairs = jnp.dot(
        normalized_input,
        key_value_weight.reshape(width, 2 * HEAD_SIZE),
        preferred_element_type=jnp.float32,
    )
    new_keys = apply_rotary(rotation_pairs[:, None, :HEAD_SIZE], token_positions)[:, 0].astype(
        jnp.bfloat16
    )
    new_values = rotation_pairs[:, HEAD_SIZE:].astype(jnp.bfloat16)
    entry = jnp.concatenate([new_keys, new_values], axis=1)

    spread, entry = lax.optimization_barrier((spread, entry))
    window_chunk = half_rows // groups
    entry_chunk = rows_new // groups
    lanes = stored.shape[1]
    second = jnp.concatenate(
        [
            jnp.take(spread.reshape(groups, window_chunk, lanes), slots, axis=0),
            entry.reshape(groups, entry_chunk, lanes),
        ],
        axis=1,
    ).reshape(groups * (window_chunk + entry_chunk), lanes)
    delivered = carry_in(second).reshape(groups, window_chunk + entry_chunk, lanes)
    window = delivered[:, :window_chunk].reshape(half_rows, lanes)
    entry_parts = delivered[:, window_chunk:]

    query_cols = query_weight.shape[2]
    heads = query_cols // HEAD_SIZE
    queries = jnp.dot(
        normalized_input,
        query_weight.reshape(width, query_cols),
        preferred_element_type=jnp.float32,
    )
    query_rotated = apply_rotary(
        queries.reshape(rows_new, heads, HEAD_SIZE), token_positions
    ).astype(jnp.bfloat16)
    factor = 1.0 / math.sqrt(HEAD_SIZE)
    rows = jnp.arange(rows_new, dtype=jnp.int32)
    new_mask = rows[None, :] <= rows[:, None]
    cycle = jnp.arange(WINDOW_LENGTH, dtype=jnp.int32)
    held = length - 1 - jnp.mod(offset - 1 - cycle, WINDOW_LENGTH)
    cache_mask = (held[None, :] >= 0) & (held[None, :] > token_positions[:, None] - WINDOW_LENGTH)
    mask_all = jnp.concatenate([cache_mask, new_mask], axis=1)
    keys_all = jnp.concatenate([window[:, :HEAD_SIZE], new_keys], axis=0)
    values_all = jnp.concatenate([window[:, HEAD_SIZE:], new_values], axis=0)

    def one_head(query_rows):
        scores = (
            jnp.einsum("qd,kd->qk", query_rows, keys_all, preferred_element_type=jnp.float32)
            * factor
        )
        scores = jnp.where(mask_all, scores, -jnp.inf)
        top = jnp.max(scores, axis=1, keepdims=True)
        powers = jnp.exp(scores - top)
        total = jnp.sum(powers, axis=1, keepdims=True)
        weights = powers.astype(jnp.bfloat16)
        summed = jnp.dot(weights, values_all, preferred_element_type=jnp.float32)
        return (summed / total).astype(jnp.bfloat16)

    outputs = lax.map(one_head, jnp.transpose(query_rotated, (1, 0, 2)))
    attended = jnp.transpose(outputs, (1, 0, 2)).reshape(rows_new, heads * HEAD_SIZE)

    arrived = carry_out(jnp.take(entry_parts, inverse, axis=0).reshape(rows_new, lanes))
    own_offset = offsets[inverse[request]]
    extended = jnp.concatenate([stored, stored[:rows_new]], axis=0)
    extended = lax.dynamic_update_slice_in_dim(extended, arrived, own_offset, axis=0)
    wrap = own_offset + rows_new - WINDOW_LENGTH
    head_rows = jnp.arange(rows_new, dtype=jnp.int32)[:, None]
    head = jnp.where(head_rows < wrap, extended[WINDOW_LENGTH:], extended[:rows_new])
    updated = jnp.concatenate([head, extended[rows_new:WINDOW_LENGTH]], axis=0)
    new_cache = updated[None, None]
    out_rows = output_weight.reshape(output_weight.shape[1], width)
    halves = lax.axis_size("tx")
    if halves == 2:
        core = lax.axis_index("tx")
        half_cols = width // halves
        sent = jnp.dot(
            attended,
            lax.dynamic_slice_in_dim(out_rows, (1 - core) * half_cols, half_cols, axis=1),
            preferred_element_type=jnp.float32,
        ).astype(jnp.bfloat16)
        received = lax.ppermute(sent, "tx", [(0, 1), (1, 0)])
        kept = jnp.dot(
            attended,
            lax.dynamic_slice_in_dim(out_rows, core * half_cols, half_cols, axis=1),
            preferred_element_type=jnp.float32,
        )
        across_cores = kept + received.astype(jnp.float32)
    else:
        partial_value = jnp.dot(attended, out_rows, preferred_element_type=jnp.float32)
        across_cores = lax.psum_scatter(partial_value, "tx", scatter_dimension=1, tiled=True)
    mixed = lax.psum_scatter(
        across_cores.astype(jnp.bfloat16), "ty", scatter_dimension=1, tiled=True
    )
    return (mixed, new_cache)


def solution(mesh):
    return jax.shard_map(
        per_device,
        mesh=mesh,
        in_specs=(
            P("dp", "tx"),
            P(None, "ty", "tx"),
            P(None, "ty", None),
            P("ty", "tx", None),
            P("dp", "ty", None, None),
            P(),
            P(),
            P(),
        ),
        out_specs=(P("dp", ("tx", "ty")), P("dp", "ty", None, None)),
        check_vma=False,
    )
```

```python
import math

import jax
import jax.numpy as jnp
from jax import lax
from jax.sharding import PartitionSpec as P

HEAD_SIZE = 64
WINDOW_LENGTH = 2048


EPS = 1e-05


def apply_rotary(values, token_positions):
    width = values.shape[-1]
    half_width = width // 2
    freqs = jnp.exp(jnp.arange(half_width, dtype=jnp.float32) * (-2.0 * math.log(10000.0) / width))
    angles = token_positions.astype(jnp.float32)[:, None] * freqs[None, :]
    cosine = jnp.cos(angles)[:, None, :]
    sine = jnp.sin(angles)[:, None, :]
    leading = values[..., :half_width]
    trailing = values[..., half_width:]
    return jnp.concatenate(
        [leading * cosine - trailing * sine, trailing * cosine + leading * sine], axis=-1
    )


def carry_in(window):
    return lax.all_to_all(window, "dp", split_axis=0, concat_axis=0, tiled=True)


def carry_out(window):
    return lax.all_to_all(window, "dp", split_axis=0, concat_axis=0, tiled=True)


def reorder(window, order, groups):
    columns = window.shape[1]
    blocks = window.reshape(groups, window.shape[0] // groups, columns)
    return jnp.take(blocks, order, axis=0).reshape(window.shape[0], columns)


def per_device(
    tokens, query_weight, key_value_weight, output_weight, cache, lengths, offsets, slots
):
    request = lax.axis_index("dp")
    groups = lax.axis_size("dp")
    stored = cache[0, 0]
    half_rows = stored.shape[0]
    spread = carry_in(stored)
    whole = lax.all_gather(tokens, "tx", axis=1, tiled=True)
    rows_new = whole.shape[0]
    width = whole.shape[1]
    floats = whole.astype(jnp.float32)
    normalized_input = (
        floats * lax.rsqrt(jnp.mean(floats * floats, axis=1, keepdims=True) + EPS)
    ).astype(jnp.bfloat16)
    owners = jnp.arange(slots.shape[0], dtype=jnp.int32)
    inverse = jnp.sum(jnp.where(slots[None, :] == owners[:, None], owners[None, :], 0), axis=1)
    length = lengths[request]
    offset = offsets[request]
    token_positions = length + jnp.arange(rows_new, dtype=jnp.int32)
    rotation_pairs = jnp.dot(
        normalized_input,
        key_value_weight.reshape(width, 2 * HEAD_SIZE),
        preferred_element_type=jnp.float32,
    )
    new_keys = apply_rotary(rotation_pairs[:, None, :HEAD_SIZE], token_positions)[:, 0].astype(
        jnp.bfloat16
    )
    new_values = rotation_pairs[:, HEAD_SIZE:].astype(jnp.bfloat16)
    entry = jnp.concatenate([new_keys, new_values], axis=1)

    window_chunk = half_rows // groups
    entry_chunk = rows_new // groups
    lanes = stored.shape[1]
    second = jnp.concatenate(
        [
            jnp.take(spread.reshape(groups, window_chunk, lanes), slots, axis=0),
            entry.reshape(groups, entry_chunk, lanes),
        ],
        axis=1,
    ).reshape(groups * (window_chunk + entry_chunk), lanes)
    delivered = carry_in(second).reshape(groups, window_chunk + entry_chunk, lanes)
    window = delivered[:, :window_chunk].reshape(half_rows, lanes)
    entry_parts = delivered[:, window_chunk:]

    query_cols = query_weight.shape[2]
    heads = query_cols // HEAD_SIZE
    queries = jnp.dot(
        normalized_input,
        query_weight.reshape(width, query_cols),
        preferred_element_type=jnp.float32,
    )
    query_rotated = apply_rotary(
        queries.reshape(rows_new, heads, HEAD_SIZE), token_positions
    ).astype(jnp.bfloat16)
    factor = 1.0 / math.sqrt(HEAD_SIZE)
    rows = jnp.arange(rows_new, dtype=jnp.int32)
    new_mask = rows[None, :] <= rows[:, None]
    cycle = jnp.arange(WINDOW_LENGTH, dtype=jnp.int32)
    held = length - 1 - jnp.mod(offset - 1 - cycle, WINDOW_LENGTH)
    cache_mask = (held[None, :] >= 0) & (held[None, :] > token_positions[:, None] - WINDOW_LENGTH)
    mask_all = jnp.concatenate([cache_mask, new_mask], axis=1)
    keys_all = jnp.concatenate([window[:, :HEAD_SIZE], new_keys], axis=0)
    values_all = jnp.concatenate([window[:, HEAD_SIZE:], new_values], axis=0)

    def one_head(query_rows):
        scores = (
            jnp.einsum("qd,kd->qk", query_rows, keys_all, preferred_element_type=jnp.float32)
            * factor
        )
        scores = jnp.where(mask_all, scores, -jnp.inf)
        top = jnp.max(scores, axis=1, keepdims=True)
        powers = jnp.exp(scores - top)
        total = jnp.sum(powers, axis=1, keepdims=True)
        weights = powers.astype(jnp.bfloat16)
        summed = jnp.dot(weights, values_all, preferred_element_type=jnp.float32)
        return (summed / total).astype(jnp.bfloat16)

    outputs = lax.map(one_head, jnp.transpose(query_rotated, (1, 0, 2)))
    attended = jnp.transpose(outputs, (1, 0, 2)).reshape(rows_new, heads * HEAD_SIZE)

    arrived = carry_out(jnp.take(entry_parts, inverse, axis=0).reshape(rows_new, lanes))
    own_offset = offsets[inverse[request]]
    extended = jnp.concatenate([stored, stored[:rows_new]], axis=0)
    extended = lax.dynamic_update_slice_in_dim(extended, arrived, own_offset, axis=0)
    wrap = own_offset + rows_new - WINDOW_LENGTH
    head_rows = jnp.arange(rows_new, dtype=jnp.int32)[:, None]
    head = jnp.where(head_rows < wrap, extended[WINDOW_LENGTH:], extended[:rows_new])
    updated = jnp.concatenate([head, extended[rows_new:WINDOW_LENGTH]], axis=0)
    new_cache = updated[None, None]
    out_rows = output_weight.reshape(output_weight.shape[1], width)
    halves = lax.axis_size("tx")
    if halves == 2:
        core = lax.axis_index("tx")
        half_cols = width // halves
        sent = jnp.dot(
            attended,
            lax.dynamic_slice_in_dim(out_rows, (1 - core) * half_cols, half_cols, axis=1),
            preferred_element_type=jnp.float32,
        ).astype(jnp.bfloat16)
        received = lax.ppermute(sent, "tx", [(0, 1), (1, 0)])
        kept = jnp.dot(
            attended,
            lax.dynamic_slice_in_dim(out_rows, core * half_cols, half_cols, axis=1),
            preferred_element_type=jnp.float32,
        )
        across_cores = kept + received.astype(jnp.float32)
    else:
        partial_value = jnp.dot(attended, out_rows, preferred_element_type=jnp.float32)
        across_cores = lax.psum_scatter(partial_value, "tx", scatter_dimension=1, tiled=True)
    mixed = lax.psum_scatter(
        across_cores.astype(jnp.bfloat16), "ty", scatter_dimension=1, tiled=True
    )
    return (mixed, new_cache)


def solution(mesh):
    return jax.shard_map(
        per_device,
        mesh=mesh,
        in_specs=(
            P("dp", "tx"),
            P(None, "ty", "tx"),
            P(None, "ty", None),
            P("ty", "tx", None),
            P("dp", "ty", None, None),
            P(),
            P(),
            P(),
        ),
        out_specs=(P("dp", ("tx", "ty")), P("dp", "ty", None, None)),
        check_vma=False,
    )
```

```python
import math

import jax
import jax.numpy as jnp
from jax import lax
from jax.sharding import PartitionSpec as P

HEAD_SIZE = 64
WINDOW_LENGTH = 2048


EPS = 1e-05


def apply_rotary(values, token_positions):
    width = values.shape[-1]
    half_width = width // 2
    freqs = jnp.exp(jnp.arange(half_width, dtype=jnp.float32) * (-2.0 * math.log(10000.0) / width))
    angles = token_positions.astype(jnp.float32)[:, None] * freqs[None, :]
    cosine = jnp.cos(angles)[:, None, :]
    sine = jnp.sin(angles)[:, None, :]
    leading = values[..., :half_width]
    trailing = values[..., half_width:]
    return jnp.concatenate(
        [leading * cosine - trailing * sine, trailing * cosine + leading * sine], axis=-1
    )


def carry_in(window):
    return lax.all_to_all(window, "dp", split_axis=0, concat_axis=0, tiled=True)


def carry_out(window):
    return lax.all_to_all(window, "dp", split_axis=0, concat_axis=0, tiled=True)


def reorder(window, order, groups):
    columns = window.shape[1]
    blocks = window.reshape(groups, window.shape[0] // groups, columns)
    return jnp.take(blocks, order, axis=0).reshape(window.shape[0], columns)


def per_device(
    tokens, query_weight, key_value_weight, output_weight, cache, lengths, offsets, slots
):
    request = lax.axis_index("dp")
    groups = lax.axis_size("dp")
    stored = cache[0, 0]
    half_rows = stored.shape[0]
    spread = carry_in(stored)
    whole = lax.all_gather(tokens, "tx", axis=1, tiled=True)
    rows_new = whole.shape[0]
    width = whole.shape[1]
    floats = whole.astype(jnp.float32)
    normalized_input = (
        floats * lax.rsqrt(jnp.mean(floats * floats, axis=1, keepdims=True) + EPS)
    ).astype(jnp.bfloat16)
    owners = jnp.arange(slots.shape[0], dtype=jnp.int32)
    inverse = jnp.sum(jnp.where(slots[None, :] == owners[:, None], owners[None, :], 0), axis=1)
    length = lengths[request]
    offset = offsets[request]
    token_positions = length + jnp.arange(rows_new, dtype=jnp.int32)
    rotation_pairs = jnp.dot(
        normalized_input,
        key_value_weight.reshape(width, 2 * HEAD_SIZE),
        preferred_element_type=jnp.float32,
    )
    new_keys = apply_rotary(rotation_pairs[:, None, :HEAD_SIZE], token_positions)[:, 0].astype(
        jnp.bfloat16
    )
    new_values = rotation_pairs[:, HEAD_SIZE:].astype(jnp.bfloat16)
    entry = jnp.concatenate([new_keys, new_values], axis=1)

    spread, entry = lax.optimization_barrier((spread, entry))
    window_chunk = half_rows // groups
    entry_chunk = rows_new // groups
    lanes = stored.shape[1]
    second = jnp.concatenate(
        [
            jnp.take(spread.reshape(groups, window_chunk, lanes), slots, axis=0),
            entry.reshape(groups, entry_chunk, lanes),
        ],
        axis=1,
    ).reshape(groups * (window_chunk + entry_chunk), lanes)
    delivered = carry_in(second).reshape(groups, window_chunk + entry_chunk, lanes)
    window = delivered[:, :window_chunk].reshape(half_rows, lanes)
    entry_parts = delivered[:, window_chunk:]

    query_cols = query_weight.shape[2]
    heads = query_cols // HEAD_SIZE
    queries = jnp.dot(
        normalized_input,
        query_weight.reshape(width, query_cols),
        preferred_element_type=jnp.float32,
    )
    query_rotated = apply_rotary(
        queries.reshape(rows_new, heads, HEAD_SIZE), token_positions
    ).astype(jnp.bfloat16)
    factor = 1.0 / math.sqrt(HEAD_SIZE)
    rows = jnp.arange(rows_new, dtype=jnp.int32)
    new_mask = rows[None, :] <= rows[:, None]
    cycle = jnp.arange(WINDOW_LENGTH, dtype=jnp.int32)
    held = length - 1 - jnp.mod(offset - 1 - cycle, WINDOW_LENGTH)
    cache_mask = (held[None, :] >= 0) & (held[None, :] > token_positions[:, None] - WINDOW_LENGTH)
    mask_all = jnp.concatenate([cache_mask, new_mask], axis=1)
    keys_all = jnp.concatenate([window[:, :HEAD_SIZE], new_keys], axis=0)
    values_all = jnp.concatenate([window[:, HEAD_SIZE:], new_values], axis=0)

    def one_head(query_rows):
        scores = (
            jnp.einsum("qd,kd->qk", query_rows, keys_all, preferred_element_type=jnp.float32)
            * factor
        )
        scores = jnp.where(mask_all, scores, -jnp.inf)
        top = jnp.max(scores, axis=1, keepdims=True)
        powers = jnp.exp(scores - top)
        total = jnp.sum(powers, axis=1, keepdims=True)
        weights = powers.astype(jnp.bfloat16)
        summed = jnp.dot(weights, values_all, preferred_element_type=jnp.float32)
        return (summed / total).astype(jnp.bfloat16)

    outputs = lax.map(one_head, jnp.transpose(query_rotated, (1, 0, 2)))
    attended = jnp.transpose(outputs, (1, 0, 2)).reshape(rows_new, heads * HEAD_SIZE)

    arrived = carry_out(jnp.take(entry_parts, inverse, axis=0).reshape(rows_new, lanes))
    own_offset = offsets[inverse[request]]
    extended = jnp.concatenate([stored, stored[:rows_new]], axis=0)
    extended = lax.dynamic_update_slice_in_dim(extended, arrived, own_offset, axis=0)
    wrap = own_offset + rows_new - WINDOW_LENGTH
    head_rows = jnp.arange(rows_new, dtype=jnp.int32)[:, None]
    head = jnp.where(head_rows < wrap, extended[WINDOW_LENGTH:], extended[:rows_new])
    updated = jnp.concatenate([head, extended[rows_new:WINDOW_LENGTH]], axis=0)
    new_cache = updated[None, None]
    out_rows = output_weight.reshape(output_weight.shape[1], width)
    halves = lax.axis_size("tx")
    if halves == 2:
        core = lax.axis_index("tx")
        half_cols = width // halves
        sent = jnp.dot(
            attended,
            lax.dynamic_slice_in_dim(out_rows, (1 - core) * half_cols, half_cols, axis=1),
            preferred_element_type=jnp.float32,
        ).astype(jnp.bfloat16)
        received = lax.ppermute(sent, "tx", [(0, 1), (1, 0)])
        kept = jnp.dot(
            attended,
            lax.dynamic_slice_in_dim(out_rows, core * half_cols, half_cols, axis=1),
            preferred_element_type=jnp.float32,
        )
        across_cores = kept + received.astype(jnp.float32)
    else:
        partial_value = jnp.dot(attended, out_rows, preferred_element_type=jnp.float32)
        across_cores = lax.psum_scatter(partial_value, "tx", scatter_dimension=1, tiled=True)
    mixed = lax.psum_scatter(
        across_cores.astype(jnp.bfloat16), "ty", scatter_dimension=1, tiled=True
    )
    return (mixed, new_cache)


def solution(mesh):
    return jax.shard_map(
        per_device,
        mesh=mesh,
        in_specs=(
            P("dp", "tx"),
            P(None, "ty", "tx"),
            P(None, "ty", None),
            P("ty", "tx", None),
            P("dp", "ty", None, None),
            P(),
            P(),
            P(),
        ),
        out_specs=(P("dp", ("tx", "ty")), P("dp", "ty", None, None)),
        check_vma=False,
    )
```

```python
import math

import jax
import jax.numpy as jnp
from jax import lax
from jax.sharding import PartitionSpec as P

HEAD_SIZE = 64
WINDOW_LENGTH = 2048


EPS = 1e-05


def apply_rotary(values, token_positions):
    width = values.shape[-1]
    half_width = width // 2
    freqs = jnp.exp(jnp.arange(half_width, dtype=jnp.float32) * (-2.0 * math.log(10000.0) / width))
    angles = token_positions.astype(jnp.float32)[:, None] * freqs[None, :]
    cosine = jnp.cos(angles)[:, None, :]
    sine = jnp.sin(angles)[:, None, :]
    leading = values[..., :half_width]
    trailing = values[..., half_width:]
    return jnp.concatenate(
        [leading * cosine - trailing * sine, trailing * cosine + leading * sine], axis=-1
    )


def carry_in(window):
    return lax.all_to_all(window, "dp", split_axis=0, concat_axis=0, tiled=True)


def carry_out(window):
    return lax.all_to_all(window, "dp", split_axis=0, concat_axis=0, tiled=True)


def reorder(window, order, groups):
    columns = window.shape[1]
    blocks = window.reshape(groups, window.shape[0] // groups, columns)
    return jnp.take(blocks, order, axis=0).reshape(window.shape[0], columns)


def per_device(
    tokens, query_weight, key_value_weight, output_weight, cache, lengths, offsets, slots
):
    request = lax.axis_index("dp")
    groups = lax.axis_size("dp")
    stored = cache[0, 0]
    half_rows = stored.shape[0]
    spread = carry_in(stored)
    whole = lax.all_gather(tokens, "tx", axis=1, tiled=True)
    rows_new = whole.shape[0]
    width = whole.shape[1]
    floats = whole.astype(jnp.float32)
    normalized_input = (
        floats * lax.rsqrt(jnp.mean(floats * floats, axis=1, keepdims=True) + EPS)
    ).astype(jnp.bfloat16)
    owners = jnp.arange(slots.shape[0], dtype=jnp.int32)
    inverse = jnp.sum(jnp.where(slots[None, :] == owners[:, None], owners[None, :], 0), axis=1)
    length = lengths[request]
    offset = offsets[request]
    token_positions = length + jnp.arange(rows_new, dtype=jnp.int32)
    rotation_pairs = jnp.dot(
        normalized_input,
        key_value_weight.reshape(width, 2 * HEAD_SIZE),
        preferred_element_type=jnp.float32,
    )
    new_keys = apply_rotary(rotation_pairs[:, None, :HEAD_SIZE], token_positions)[:, 0].astype(
        jnp.bfloat16
    )
    new_values = rotation_pairs[:, HEAD_SIZE:].astype(jnp.bfloat16)
    entry = jnp.concatenate([new_keys, new_values], axis=1)

    spread, entry = lax.optimization_barrier((spread, entry))
    window_chunk = half_rows // groups
    entry_chunk = rows_new // groups
    lanes = stored.shape[1]
    second = jnp.concatenate(
        [
            jnp.take(spread.reshape(groups, window_chunk, lanes), slots, axis=0),
            entry.reshape(groups, entry_chunk, lanes),
        ],
        axis=1,
    ).reshape(groups * (window_chunk + entry_chunk), lanes)
    delivered = carry_in(second).reshape(groups, window_chunk + entry_chunk, lanes)
    window = delivered[:, :window_chunk].reshape(half_rows, lanes)
    entry_parts = delivered[:, window_chunk:]

    query_cols = query_weight.shape[2]
    heads = query_cols // HEAD_SIZE
    queries = jnp.dot(
        normalized_input,
        query_weight.reshape(width, query_cols),
        preferred_element_type=jnp.float32,
    )
    query_rotated = apply_rotary(
        queries.reshape(rows_new, heads, HEAD_SIZE), token_positions
    ).astype(jnp.bfloat16)
    factor = 1.0 / math.sqrt(HEAD_SIZE)
    rows = jnp.arange(rows_new, dtype=jnp.int32)
    new_mask = rows[None, :] <= rows[:, None]
    cycle = jnp.arange(WINDOW_LENGTH, dtype=jnp.int32)
    held = length - 1 - jnp.mod(offset - 1 - cycle, WINDOW_LENGTH)
    cache_mask = (held[None, :] >= 0) & (held[None, :] > token_positions[:, None] - WINDOW_LENGTH)
    window_keys = window[:, :HEAD_SIZE]
    window_values = window[:, HEAD_SIZE:]

    def one_head(query_rows):
        old_scores = (
            jnp.einsum("qd,kd->qk", query_rows, window_keys, preferred_element_type=jnp.float32)
            * factor
        )
        new_scores = (
            jnp.einsum("qd,kd->qk", query_rows, new_keys, preferred_element_type=jnp.float32)
            * factor
        )
        old_scores = jnp.where(cache_mask, old_scores, -jnp.inf)
        new_scores = jnp.where(new_mask, new_scores, -jnp.inf)
        top = jnp.maximum(
            jnp.max(old_scores, axis=1, keepdims=True), jnp.max(new_scores, axis=1, keepdims=True)
        )
        old_powers = jnp.exp(old_scores - top)
        new_powers = jnp.exp(new_scores - top)
        total = jnp.sum(old_powers, axis=1, keepdims=True) + jnp.sum(
            new_powers, axis=1, keepdims=True
        )
        summed = jnp.dot(
            old_powers.astype(jnp.bfloat16), window_values, preferred_element_type=jnp.float32
        ) + jnp.dot(new_powers.astype(jnp.bfloat16), new_values, preferred_element_type=jnp.float32)
        return (summed / total).astype(jnp.bfloat16)

    outputs = lax.map(one_head, jnp.transpose(query_rotated, (1, 0, 2)))
    attended = jnp.transpose(outputs, (1, 0, 2)).reshape(rows_new, heads * HEAD_SIZE)

    arrived = carry_out(jnp.take(entry_parts, inverse, axis=0).reshape(rows_new, lanes))
    own_offset = offsets[inverse[request]]
    extended = jnp.concatenate([stored, stored[:rows_new]], axis=0)
    extended = lax.dynamic_update_slice_in_dim(extended, arrived, own_offset, axis=0)
    wrap = own_offset + rows_new - WINDOW_LENGTH
    head_rows = jnp.arange(rows_new, dtype=jnp.int32)[:, None]
    head = jnp.where(head_rows < wrap, extended[WINDOW_LENGTH:], extended[:rows_new])
    updated = jnp.concatenate([head, extended[rows_new:WINDOW_LENGTH]], axis=0)
    new_cache = updated[None, None]
    out_rows = output_weight.reshape(output_weight.shape[1], width)
    halves = lax.axis_size("tx")
    if halves == 2:
        core = lax.axis_index("tx")
        half_cols = width // halves
        sent = jnp.dot(
            attended,
            lax.dynamic_slice_in_dim(out_rows, (1 - core) * half_cols, half_cols, axis=1),
            preferred_element_type=jnp.float32,
        ).astype(jnp.bfloat16)
        received = lax.ppermute(sent, "tx", [(0, 1), (1, 0)])
        kept = jnp.dot(
            attended,
            lax.dynamic_slice_in_dim(out_rows, core * half_cols, half_cols, axis=1),
            preferred_element_type=jnp.float32,
        )
        across_cores = kept + received.astype(jnp.float32)
    else:
        partial_value = jnp.dot(attended, out_rows, preferred_element_type=jnp.float32)
        across_cores = lax.psum_scatter(partial_value, "tx", scatter_dimension=1, tiled=True)
    mixed = lax.psum_scatter(
        across_cores.astype(jnp.bfloat16), "ty", scatter_dimension=1, tiled=True
    )
    return (mixed, new_cache)


def solution(mesh):
    return jax.shard_map(
        per_device,
        mesh=mesh,
        in_specs=(
            P("dp", "tx"),
            P(None, "ty", "tx"),
            P(None, "ty", None),
            P("ty", "tx", None),
            P("dp", "ty", None, None),
            P(),
            P(),
            P(),
        ),
        out_specs=(P("dp", ("tx", "ty")), P("dp", "ty", None, None)),
        check_vma=False,
    )
```

```python
import math

import jax
import jax.numpy as jnp
from jax import lax
from jax.sharding import PartitionSpec as P

HEAD_SIZE = 64
WINDOW_LENGTH = 2048


EPS = 1e-05


def apply_rotary(values, token_positions):
    width = values.shape[-1]
    half_width = width // 2
    freqs = jnp.exp(jnp.arange(half_width, dtype=jnp.float32) * (-2.0 * math.log(10000.0) / width))
    angles = token_positions.astype(jnp.float32)[:, None] * freqs[None, :]
    cosine = jnp.cos(angles)[:, None, :]
    sine = jnp.sin(angles)[:, None, :]
    leading = values[..., :half_width]
    trailing = values[..., half_width:]
    return jnp.concatenate(
        [leading * cosine - trailing * sine, trailing * cosine + leading * sine], axis=-1
    )


def carry_in(window):
    return lax.all_to_all(window, "dp", split_axis=0, concat_axis=0, tiled=True)


def carry_out(window):
    return lax.all_to_all(window, "dp", split_axis=0, concat_axis=0, tiled=True)


def reorder(window, order, groups):
    columns = window.shape[1]
    blocks = window.reshape(groups, window.shape[0] // groups, columns)
    return jnp.take(blocks, order, axis=0).reshape(window.shape[0], columns)


def per_device(
    tokens, query_weight, key_value_weight, output_weight, cache, lengths, offsets, slots
):
    request = lax.axis_index("dp")
    groups = lax.axis_size("dp")
    stored = cache[0, 0]
    half_rows = stored.shape[0]
    spread = carry_in(stored)
    whole = lax.all_gather(tokens, "tx", axis=1, tiled=True)
    rows_new = whole.shape[0]
    width = whole.shape[1]
    floats = whole.astype(jnp.float32)
    normalized_input = (
        floats * lax.rsqrt(jnp.mean(floats * floats, axis=1, keepdims=True) + EPS)
    ).astype(jnp.bfloat16)
    owners = jnp.arange(slots.shape[0], dtype=jnp.int32)
    inverse = jnp.sum(jnp.where(slots[None, :] == owners[:, None], owners[None, :], 0), axis=1)
    length = lengths[request]
    offset = offsets[request]
    token_positions = length + jnp.arange(rows_new, dtype=jnp.int32)
    rotation_pairs = jnp.dot(
        normalized_input,
        key_value_weight.reshape(width, 2 * HEAD_SIZE),
        preferred_element_type=jnp.float32,
    )
    new_keys = apply_rotary(rotation_pairs[:, None, :HEAD_SIZE], token_positions)[:, 0].astype(
        jnp.bfloat16
    )
    new_values = rotation_pairs[:, HEAD_SIZE:].astype(jnp.bfloat16)
    entry = jnp.concatenate([new_keys, new_values], axis=1)

    spread, entry = lax.optimization_barrier((spread, entry))
    window_chunk = half_rows // groups
    entry_chunk = rows_new // groups
    lanes = stored.shape[1]
    second = jnp.concatenate(
        [
            jnp.take(spread.reshape(groups, window_chunk, lanes), slots, axis=0),
            entry.reshape(groups, entry_chunk, lanes),
        ],
        axis=1,
    ).reshape(groups * (window_chunk + entry_chunk), lanes)
    delivered = carry_in(second).reshape(groups, window_chunk + entry_chunk, lanes)
    window = delivered[:, :window_chunk].reshape(half_rows, lanes)
    entry_parts = delivered[:, window_chunk:]

    query_cols = query_weight.shape[2]
    heads = query_cols // HEAD_SIZE
    queries = jnp.dot(
        normalized_input,
        query_weight.reshape(width, query_cols),
        preferred_element_type=jnp.float32,
    )
    query_rotated = apply_rotary(
        queries.reshape(rows_new, heads, HEAD_SIZE), token_positions
    ).astype(jnp.bfloat16)
    factor = 1.0 / math.sqrt(HEAD_SIZE)
    rows = jnp.arange(rows_new, dtype=jnp.int32)
    new_mask = rows[None, :] <= rows[:, None]
    cycle = jnp.arange(WINDOW_LENGTH, dtype=jnp.int32)
    held = length - 1 - jnp.mod(offset - 1 - cycle, WINDOW_LENGTH)
    cache_mask = (held[None, :] >= 0) & (held[None, :] > token_positions[:, None] - WINDOW_LENGTH)
    window_keys = window[:, :HEAD_SIZE]
    window_values = window[:, HEAD_SIZE:]

    def one_head(query_rows):
        old_scores = (
            jnp.einsum("qd,kd->qk", query_rows, window_keys, preferred_element_type=jnp.float32)
            * factor
        )
        new_scores = (
            jnp.einsum("qd,kd->qk", query_rows, new_keys, preferred_element_type=jnp.float32)
            * factor
        )
        old_scores = jnp.where(cache_mask, old_scores, -jnp.inf)
        new_scores = jnp.where(new_mask, new_scores, -jnp.inf)
        top = jnp.maximum(
            jnp.max(old_scores, axis=1, keepdims=True), jnp.max(new_scores, axis=1, keepdims=True)
        )
        old_powers = jnp.exp(old_scores - top)
        new_powers = jnp.exp(new_scores - top)
        total = jnp.sum(old_powers, axis=1, keepdims=True) + jnp.sum(
            new_powers, axis=1, keepdims=True
        )
        summed = jnp.dot(
            old_powers.astype(jnp.bfloat16), window_values, preferred_element_type=jnp.float32
        ) + jnp.dot(new_powers.astype(jnp.bfloat16), new_values, preferred_element_type=jnp.float32)
        return (summed / total).astype(jnp.bfloat16)

    outputs = jnp.stack([one_head(query_rotated[:, h]) for h in range(heads)])
    attended = jnp.transpose(outputs, (1, 0, 2)).reshape(rows_new, heads * HEAD_SIZE)

    arrived = carry_out(jnp.take(entry_parts, inverse, axis=0).reshape(rows_new, lanes))
    own_offset = offsets[inverse[request]]
    extended = jnp.concatenate([stored, stored[:rows_new]], axis=0)
    extended = lax.dynamic_update_slice_in_dim(extended, arrived, own_offset, axis=0)
    wrap = own_offset + rows_new - WINDOW_LENGTH
    head_rows = jnp.arange(rows_new, dtype=jnp.int32)[:, None]
    head = jnp.where(head_rows < wrap, extended[WINDOW_LENGTH:], extended[:rows_new])
    updated = jnp.concatenate([head, extended[rows_new:WINDOW_LENGTH]], axis=0)
    new_cache = updated[None, None]
    out_rows = output_weight.reshape(output_weight.shape[1], width)
    halves = lax.axis_size("tx")
    if halves == 2:
        core = lax.axis_index("tx")
        half_cols = width // halves
        sent = jnp.dot(
            attended,
            lax.dynamic_slice_in_dim(out_rows, (1 - core) * half_cols, half_cols, axis=1),
            preferred_element_type=jnp.float32,
        ).astype(jnp.bfloat16)
        received = lax.ppermute(sent, "tx", [(0, 1), (1, 0)])
        kept = jnp.dot(
            attended,
            lax.dynamic_slice_in_dim(out_rows, core * half_cols, half_cols, axis=1),
            preferred_element_type=jnp.float32,
        )
        across_cores = kept + received.astype(jnp.float32)
    else:
        partial_value = jnp.dot(attended, out_rows, preferred_element_type=jnp.float32)
        across_cores = lax.psum_scatter(partial_value, "tx", scatter_dimension=1, tiled=True)
    mixed = lax.psum_scatter(
        across_cores.astype(jnp.bfloat16), "ty", scatter_dimension=1, tiled=True
    )
    return (mixed, new_cache)


def solution(mesh):
    return jax.shard_map(
        per_device,
        mesh=mesh,
        in_specs=(
            P("dp", "tx"),
            P(None, "ty", "tx"),
            P(None, "ty", None),
            P("ty", "tx", None),
            P("dp", "ty", None, None),
            P(),
            P(),
            P(),
        ),
        out_specs=(P("dp", ("tx", "ty")), P("dp", "ty", None, None)),
        check_vma=False,
    )
```

```python
import math

import jax
import jax.numpy as jnp
from jax import lax
from jax.sharding import PartitionSpec as P

HEAD_SIZE = 64
WINDOW_LENGTH = 2048


EPS = 1e-05


def apply_rotary(values, token_positions):
    width = values.shape[-1]
    half_width = width // 2
    freqs = jnp.exp(jnp.arange(half_width, dtype=jnp.float32) * (-2.0 * math.log(10000.0) / width))
    angles = token_positions.astype(jnp.float32)[:, None] * freqs[None, :]
    cosine = jnp.cos(angles)[:, None, :]
    sine = jnp.sin(angles)[:, None, :]
    leading = values[..., :half_width]
    trailing = values[..., half_width:]
    return jnp.concatenate(
        [leading * cosine - trailing * sine, trailing * cosine + leading * sine], axis=-1
    )


def carry_in(window):
    return lax.all_to_all(window, "dp", split_axis=0, concat_axis=0, tiled=True)


def carry_out(window):
    return lax.all_to_all(window, "dp", split_axis=0, concat_axis=0, tiled=True)


def reorder(window, order, groups):
    columns = window.shape[1]
    blocks = window.reshape(groups, window.shape[0] // groups, columns)
    return jnp.take(blocks, order, axis=0).reshape(window.shape[0], columns)


def per_device(
    tokens, query_weight, key_value_weight, output_weight, cache, lengths, offsets, slots
):
    request = lax.axis_index("dp")
    groups = lax.axis_size("dp")
    stored = cache[0, 0]
    half_rows = stored.shape[0]
    spread = carry_in(stored)
    whole = lax.all_gather(tokens, "tx", axis=1, tiled=True)
    rows_new = whole.shape[0]
    width = whole.shape[1]
    floats = whole.astype(jnp.float32)
    normalized_input = (
        floats * lax.rsqrt(jnp.mean(floats * floats, axis=1, keepdims=True) + EPS)
    ).astype(jnp.bfloat16)
    owners = jnp.arange(slots.shape[0], dtype=jnp.int32)
    inverse = jnp.sum(jnp.where(slots[None, :] == owners[:, None], owners[None, :], 0), axis=1)
    length = lengths[request]
    offset = offsets[request]
    token_positions = length + jnp.arange(rows_new, dtype=jnp.int32)
    rotation_pairs = jnp.dot(
        normalized_input,
        key_value_weight.reshape(width, 2 * HEAD_SIZE),
        preferred_element_type=jnp.float32,
    )
    new_keys = apply_rotary(rotation_pairs[:, None, :HEAD_SIZE], token_positions)[:, 0].astype(
        jnp.bfloat16
    )
    new_values = rotation_pairs[:, HEAD_SIZE:].astype(jnp.bfloat16)
    entry = jnp.concatenate([new_keys, new_values], axis=1)

    spread, entry = lax.optimization_barrier((spread, entry))
    window_chunk = half_rows // groups
    entry_chunk = rows_new // groups
    lanes = stored.shape[1]
    second = jnp.concatenate(
        [
            jnp.take(spread.reshape(groups, window_chunk, lanes), slots, axis=0),
            entry.reshape(groups, entry_chunk, lanes),
        ],
        axis=1,
    ).reshape(groups * (window_chunk + entry_chunk), lanes)
    delivered = carry_in(second).reshape(groups, window_chunk + entry_chunk, lanes)
    window = delivered[:, :window_chunk].reshape(half_rows, lanes)
    entry_parts = delivered[:, window_chunk:]

    query_cols = query_weight.shape[2]
    heads = query_cols // HEAD_SIZE
    queries = jnp.dot(
        normalized_input,
        query_weight.reshape(width, query_cols),
        preferred_element_type=jnp.float32,
    )
    query_rotated = apply_rotary(
        queries.reshape(rows_new, heads, HEAD_SIZE), token_positions
    ).astype(jnp.bfloat16)
    factor = 1.0 / math.sqrt(HEAD_SIZE)
    rows = jnp.arange(rows_new, dtype=jnp.int32)
    new_mask = rows[None, :] <= rows[:, None]
    cycle = jnp.arange(WINDOW_LENGTH, dtype=jnp.int32)
    held = length - 1 - jnp.mod(offset - 1 - cycle, WINDOW_LENGTH)
    cache_mask = (held[None, :] >= 0) & (held[None, :] > token_positions[:, None] - WINDOW_LENGTH)
    window_keys = window[:, :HEAD_SIZE]
    window_values = window[:, HEAD_SIZE:]

    def one_head(query_rows):
        old_scores = (
            jnp.einsum("qd,kd->qk", query_rows, window_keys, preferred_element_type=jnp.float32)
            * factor
        )
        new_scores = (
            jnp.einsum("qd,kd->qk", query_rows, new_keys, preferred_element_type=jnp.float32)
            * factor
        )
        old_scores = jnp.where(cache_mask, old_scores, -jnp.inf)
        new_scores = jnp.where(new_mask, new_scores, -jnp.inf)
        top = jnp.maximum(
            jnp.max(old_scores, axis=1, keepdims=True), jnp.max(new_scores, axis=1, keepdims=True)
        )
        old_powers = jnp.exp(old_scores - top)
        new_powers = jnp.exp(new_scores - top)
        total = jnp.sum(old_powers, axis=1, keepdims=True) + jnp.sum(
            new_powers, axis=1, keepdims=True
        )
        summed = jnp.dot(
            old_powers.astype(jnp.bfloat16), window_values, preferred_element_type=jnp.float32
        ) + jnp.dot(new_powers.astype(jnp.bfloat16), new_values, preferred_element_type=jnp.float32)
        return (summed / total).astype(jnp.bfloat16)

    outputs = lax.map(one_head, jnp.transpose(query_rotated, (1, 0, 2)))
    attended = jnp.transpose(outputs, (1, 0, 2)).reshape(rows_new, heads * HEAD_SIZE)

    out_rows = output_weight.reshape(output_weight.shape[1], width)
    sorted_entries = jnp.take(entry_parts, inverse, axis=0).reshape(rows_new, lanes)
    halves = lax.axis_size("tx")
    if halves == 2:
        core = lax.axis_index("tx")
        half_cols = width // halves
        sent = jnp.dot(
            attended,
            lax.dynamic_slice_in_dim(out_rows, (1 - core) * half_cols, half_cols, axis=1),
            preferred_element_type=jnp.float32,
        ).astype(jnp.bfloat16)
        received = lax.ppermute(sent, "tx", [(0, 1), (1, 0)])
        sorted_entries, received = lax.optimization_barrier((sorted_entries, received))
        kept = jnp.dot(
            attended,
            lax.dynamic_slice_in_dim(out_rows, core * half_cols, half_cols, axis=1),
            preferred_element_type=jnp.float32,
        )
        across_cores = kept + received.astype(jnp.float32)
    else:
        partial_value = jnp.dot(attended, out_rows, preferred_element_type=jnp.float32)
        across_cores = lax.psum_scatter(partial_value, "tx", scatter_dimension=1, tiled=True)
    arrived = carry_out(sorted_entries)
    own_offset = offsets[inverse[request]]
    extended = jnp.concatenate([stored, stored[:rows_new]], axis=0)
    extended = lax.dynamic_update_slice_in_dim(extended, arrived, own_offset, axis=0)
    wrap = own_offset + rows_new - WINDOW_LENGTH
    head_rows = jnp.arange(rows_new, dtype=jnp.int32)[:, None]
    head = jnp.where(head_rows < wrap, extended[WINDOW_LENGTH:], extended[:rows_new])
    updated = jnp.concatenate([head, extended[rows_new:WINDOW_LENGTH]], axis=0)
    new_cache = updated[None, None]
    mixed = lax.psum_scatter(
        across_cores.astype(jnp.bfloat16), "ty", scatter_dimension=1, tiled=True
    )
    return (mixed, new_cache)


def solution(mesh):
    return jax.shard_map(
        per_device,
        mesh=mesh,
        in_specs=(
            P("dp", "tx"),
            P(None, "ty", "tx"),
            P(None, "ty", None),
            P("ty", "tx", None),
            P("dp", "ty", None, None),
            P(),
            P(),
            P(),
        ),
        out_specs=(P("dp", ("tx", "ty")), P("dp", "ty", None, None)),
        check_vma=False,
    )
```

```python
import math

import jax
import jax.numpy as jnp
from jax import lax
from jax.sharding import PartitionSpec as P

HEAD_SIZE = 64
WINDOW_LENGTH = 2048


EPS = 1e-05


def apply_rotary(values, token_positions):
    width = values.shape[-1]
    half_width = width // 2
    freqs = jnp.exp(jnp.arange(half_width, dtype=jnp.float32) * (-2.0 * math.log(10000.0) / width))
    angles = token_positions.astype(jnp.float32)[:, None] * freqs[None, :]
    cosine = jnp.cos(angles)[:, None, :]
    sine = jnp.sin(angles)[:, None, :]
    leading = values[..., :half_width]
    trailing = values[..., half_width:]
    return jnp.concatenate(
        [leading * cosine - trailing * sine, trailing * cosine + leading * sine], axis=-1
    )


def carry_in(window):
    return lax.all_to_all(window, "dp", split_axis=0, concat_axis=0, tiled=True)


def carry_out(window):
    return lax.all_to_all(window, "dp", split_axis=0, concat_axis=0, tiled=True)


def reorder(window, order, groups):
    columns = window.shape[1]
    blocks = window.reshape(groups, window.shape[0] // groups, columns)
    return jnp.take(blocks, order, axis=0).reshape(window.shape[0], columns)


def per_device(
    tokens, query_weight, key_value_weight, output_weight, cache, lengths, offsets, slots
):
    request = lax.axis_index("dp")
    groups = lax.axis_size("dp")
    stored = cache[0, 0]
    halves = lax.axis_size("tx")
    core = lax.axis_index("tx")
    half_rows = stored.shape[0] // halves
    mine = lax.dynamic_slice_in_dim(stored, core * half_rows, half_rows, axis=0)
    spread = carry_in(mine)
    whole = lax.all_gather(tokens, "tx", axis=1, tiled=True)
    rows_new = whole.shape[0]
    width = whole.shape[1]
    floats = whole.astype(jnp.float32)
    normalized_input = (
        floats * lax.rsqrt(jnp.mean(floats * floats, axis=1, keepdims=True) + EPS)
    ).astype(jnp.bfloat16)
    owners = jnp.arange(slots.shape[0], dtype=jnp.int32)
    inverse = jnp.sum(jnp.where(slots[None, :] == owners[:, None], owners[None, :], 0), axis=1)
    length = lengths[request]
    offset = offsets[request]
    token_positions = length + jnp.arange(rows_new, dtype=jnp.int32)
    rotation_pairs = jnp.dot(
        normalized_input,
        key_value_weight.reshape(width, 2 * HEAD_SIZE),
        preferred_element_type=jnp.float32,
    )
    new_keys = apply_rotary(rotation_pairs[:, None, :HEAD_SIZE], token_positions)[:, 0].astype(
        jnp.bfloat16
    )
    new_values = rotation_pairs[:, HEAD_SIZE:].astype(jnp.bfloat16)
    entry = jnp.concatenate([new_keys, new_values], axis=1)

    spread, entry = lax.optimization_barrier((spread, entry))
    window_chunk = half_rows // groups
    entry_chunk = rows_new // groups
    lanes = stored.shape[1]
    second = jnp.concatenate(
        [
            jnp.take(spread.reshape(groups, window_chunk, lanes), slots, axis=0),
            entry.reshape(groups, entry_chunk, lanes),
        ],
        axis=1,
    ).reshape(groups * (window_chunk + entry_chunk), lanes)
    delivered = carry_in(second).reshape(groups, window_chunk + entry_chunk, lanes)
    window_part = delivered[:, :window_chunk].reshape(half_rows, lanes)
    if halves == 2:
        other = lax.ppermute(window_part, "tx", [(0, 1), (1, 0)])
        window = jnp.where(
            core == 0,
            jnp.concatenate([window_part, other], axis=0),
            jnp.concatenate([other, window_part], axis=0),
        )
    else:
        window = lax.all_gather(window_part, "tx", axis=0, tiled=True)
    entry_parts = delivered[:, window_chunk:]

    query_cols = query_weight.shape[2]
    heads = query_cols // HEAD_SIZE
    queries = jnp.dot(
        normalized_input,
        query_weight.reshape(width, query_cols),
        preferred_element_type=jnp.float32,
    )
    query_rotated = apply_rotary(
        queries.reshape(rows_new, heads, HEAD_SIZE), token_positions
    ).astype(jnp.bfloat16)
    factor = 1.0 / math.sqrt(HEAD_SIZE)
    rows = jnp.arange(rows_new, dtype=jnp.int32)
    new_mask = rows[None, :] <= rows[:, None]
    cycle = jnp.arange(WINDOW_LENGTH, dtype=jnp.int32)
    held = length - 1 - jnp.mod(offset - 1 - cycle, WINDOW_LENGTH)
    cache_mask = (held[None, :] >= 0) & (held[None, :] > token_positions[:, None] - WINDOW_LENGTH)
    window_keys = window[:, :HEAD_SIZE]
    window_values = window[:, HEAD_SIZE:]

    def one_head(query_rows):
        old_scores = (
            jnp.einsum("qd,kd->qk", query_rows, window_keys, preferred_element_type=jnp.float32)
            * factor
        )
        new_scores = (
            jnp.einsum("qd,kd->qk", query_rows, new_keys, preferred_element_type=jnp.float32)
            * factor
        )
        old_scores = jnp.where(cache_mask, old_scores, -jnp.inf)
        new_scores = jnp.where(new_mask, new_scores, -jnp.inf)
        top = jnp.maximum(
            jnp.max(old_scores, axis=1, keepdims=True), jnp.max(new_scores, axis=1, keepdims=True)
        )
        old_powers = jnp.exp(old_scores - top)
        new_powers = jnp.exp(new_scores - top)
        total = jnp.sum(old_powers, axis=1, keepdims=True) + jnp.sum(
            new_powers, axis=1, keepdims=True
        )
        summed = jnp.dot(
            old_powers.astype(jnp.bfloat16), window_values, preferred_element_type=jnp.float32
        ) + jnp.dot(new_powers.astype(jnp.bfloat16), new_values, preferred_element_type=jnp.float32)
        return (summed / total).astype(jnp.bfloat16)

    outputs = lax.map(one_head, jnp.transpose(query_rotated, (1, 0, 2)))
    attended = jnp.transpose(outputs, (1, 0, 2)).reshape(rows_new, heads * HEAD_SIZE)

    arrived = carry_out(jnp.take(entry_parts, inverse, axis=0).reshape(rows_new, lanes))
    own_offset = offsets[inverse[request]]
    extended = jnp.concatenate([stored, stored[:rows_new]], axis=0)
    extended = lax.dynamic_update_slice_in_dim(extended, arrived, own_offset, axis=0)
    wrap = own_offset + rows_new - WINDOW_LENGTH
    head_rows = jnp.arange(rows_new, dtype=jnp.int32)[:, None]
    head = jnp.where(head_rows < wrap, extended[WINDOW_LENGTH:], extended[:rows_new])
    updated = jnp.concatenate([head, extended[rows_new:WINDOW_LENGTH]], axis=0)
    new_cache = updated[None, None]
    out_rows = output_weight.reshape(output_weight.shape[1], width)
    halves = lax.axis_size("tx")
    if halves == 2:
        core = lax.axis_index("tx")
        half_cols = width // halves
        sent = jnp.dot(
            attended,
            lax.dynamic_slice_in_dim(out_rows, (1 - core) * half_cols, half_cols, axis=1),
            preferred_element_type=jnp.float32,
        ).astype(jnp.bfloat16)
        received = lax.ppermute(sent, "tx", [(0, 1), (1, 0)])
        kept = jnp.dot(
            attended,
            lax.dynamic_slice_in_dim(out_rows, core * half_cols, half_cols, axis=1),
            preferred_element_type=jnp.float32,
        )
        across_cores = kept + received.astype(jnp.float32)
    else:
        partial_value = jnp.dot(attended, out_rows, preferred_element_type=jnp.float32)
        across_cores = lax.psum_scatter(partial_value, "tx", scatter_dimension=1, tiled=True)
    mixed = lax.psum_scatter(
        across_cores.astype(jnp.bfloat16), "ty", scatter_dimension=1, tiled=True
    )
    return (mixed, new_cache)


def solution(mesh):
    return jax.shard_map(
        per_device,
        mesh=mesh,
        in_specs=(
            P("dp", "tx"),
            P(None, "ty", "tx"),
            P(None, "ty", None),
            P("ty", "tx", None),
            P("dp", "ty", None, None),
            P(),
            P(),
            P(),
        ),
        out_specs=(P("dp", ("tx", "ty")), P("dp", "ty", None, None)),
        check_vma=False,
    )
```

```python
import math

import jax
import jax.numpy as jnp
from jax import lax
from jax.sharding import PartitionSpec as P

HEAD_SIZE = 64
WINDOW_LENGTH = 2048


EPS = 1e-05


def apply_rotary(values, token_positions):
    width = values.shape[-1]
    half_width = width // 2
    freqs = jnp.exp(jnp.arange(half_width, dtype=jnp.float32) * (-2.0 * math.log(10000.0) / width))
    angles = token_positions.astype(jnp.float32)[:, None] * freqs[None, :]
    cosine = jnp.cos(angles)[:, None, :]
    sine = jnp.sin(angles)[:, None, :]
    leading = values[..., :half_width]
    trailing = values[..., half_width:]
    return jnp.concatenate(
        [leading * cosine - trailing * sine, trailing * cosine + leading * sine], axis=-1
    )


def carry_in(window):
    return lax.all_to_all(window, "dp", split_axis=0, concat_axis=0, tiled=True)


def carry_out(window):
    return lax.all_to_all(window, "dp", split_axis=0, concat_axis=0, tiled=True)


def reorder(window, order, groups):
    columns = window.shape[1]
    blocks = window.reshape(groups, window.shape[0] // groups, columns)
    return jnp.take(blocks, order, axis=0).reshape(window.shape[0], columns)


def per_device(
    tokens, query_weight, key_value_weight, output_weight, cache, lengths, offsets, slots
):
    request = lax.axis_index("dp")
    groups = lax.axis_size("dp")
    stored = cache[0, 0]
    half_rows = stored.shape[0]
    spread = carry_in(stored)
    whole = lax.all_gather(tokens, "tx", axis=1, tiled=True)
    rows_new = whole.shape[0]
    width = whole.shape[1]
    floats = whole.astype(jnp.float32)
    normalized_input = (
        floats * lax.rsqrt(jnp.mean(floats * floats, axis=1, keepdims=True) + EPS)
    ).astype(jnp.bfloat16)
    owners = jnp.arange(slots.shape[0], dtype=jnp.int32)
    inverse = jnp.sum(jnp.where(slots[None, :] == owners[:, None], owners[None, :], 0), axis=1)
    length = lengths[request]
    offset = offsets[request]
    token_positions = length + jnp.arange(rows_new, dtype=jnp.int32)
    rotation_pairs = jnp.dot(
        normalized_input,
        key_value_weight.reshape(width, 2 * HEAD_SIZE),
        preferred_element_type=jnp.float32,
    )
    new_keys = apply_rotary(rotation_pairs[:, None, :HEAD_SIZE], token_positions)[:, 0].astype(
        jnp.bfloat16
    )
    new_values = rotation_pairs[:, HEAD_SIZE:].astype(jnp.bfloat16)
    entry = jnp.concatenate([new_keys, new_values], axis=1)

    spread, entry = lax.optimization_barrier((spread, entry))
    window_chunk = half_rows // groups
    entry_chunk = rows_new // groups
    lanes = stored.shape[1]
    second = jnp.concatenate(
        [
            jnp.take(spread.reshape(groups, window_chunk, lanes), slots, axis=0),
            entry.reshape(groups, entry_chunk, lanes),
        ],
        axis=1,
    ).reshape(groups * (window_chunk + entry_chunk), lanes)
    delivered = carry_in(second).reshape(groups, window_chunk + entry_chunk, lanes)
    window = delivered[:, :window_chunk].reshape(half_rows, lanes)
    entry_parts = delivered[:, window_chunk:]

    query_cols = query_weight.shape[2]
    heads = query_cols // HEAD_SIZE
    queries = jnp.dot(
        normalized_input,
        query_weight.reshape(width, query_cols),
        preferred_element_type=jnp.float32,
    )
    query_rotated = apply_rotary(
        queries.reshape(rows_new, heads, HEAD_SIZE), token_positions
    ).astype(jnp.bfloat16)
    factor = 1.0 / math.sqrt(HEAD_SIZE)
    rows = jnp.arange(rows_new, dtype=jnp.int32)
    new_mask = rows[None, :] <= rows[:, None]
    cycle = jnp.arange(WINDOW_LENGTH, dtype=jnp.int32)
    held = length - 1 - jnp.mod(offset - 1 - cycle, WINDOW_LENGTH)
    cache_mask = (held[None, :] >= 0) & (held[None, :] > token_positions[:, None] - WINDOW_LENGTH)
    window_keys = window[:, :HEAD_SIZE]
    window_values = window[:, HEAD_SIZE:]

    def one_head(query_rows):
        old_scores = (
            jnp.einsum("qd,kd->qk", query_rows, window_keys, preferred_element_type=jnp.float32)
            * factor
        )
        new_scores = (
            jnp.einsum("qd,kd->qk", query_rows, new_keys, preferred_element_type=jnp.float32)
            * factor
        )
        old_scores = jnp.where(cache_mask, old_scores, -jnp.inf)
        new_scores = jnp.where(new_mask, new_scores, -jnp.inf)
        top = jnp.maximum(
            jnp.max(old_scores, axis=1, keepdims=True), jnp.max(new_scores, axis=1, keepdims=True)
        )
        old_powers = jnp.exp(old_scores - top)
        new_powers = jnp.exp(new_scores - top)
        total = jnp.sum(old_powers, axis=1, keepdims=True) + jnp.sum(
            new_powers, axis=1, keepdims=True
        )
        summed = jnp.dot(
            old_powers.astype(jnp.bfloat16), window_values, preferred_element_type=jnp.float32
        ) + jnp.dot(new_powers.astype(jnp.bfloat16), new_values, preferred_element_type=jnp.float32)
        return (summed / total).astype(jnp.bfloat16)

    outputs = lax.map(one_head, jnp.transpose(query_rotated, (1, 0, 2)))
    attended = jnp.transpose(outputs, (1, 0, 2)).reshape(rows_new, heads * HEAD_SIZE)

    arrived = carry_out(jnp.take(entry_parts, inverse, axis=0).reshape(rows_new, lanes))
    own_offset = offsets[inverse[request]]
    extended = jnp.concatenate([stored, stored[:rows_new]], axis=0)
    extended = lax.dynamic_update_slice_in_dim(extended, arrived, own_offset, axis=0)
    wrap = own_offset + rows_new - WINDOW_LENGTH
    head_rows = jnp.arange(rows_new, dtype=jnp.int32)[:, None]
    head = jnp.where(head_rows < wrap, extended[WINDOW_LENGTH:], extended[:rows_new])
    updated = jnp.concatenate([head, extended[rows_new:WINDOW_LENGTH]], axis=0)
    new_cache = updated[None, None]
    out_rows = output_weight.reshape(output_weight.shape[1], width)
    halves = lax.axis_size("tx")
    if halves == 2:
        core = lax.axis_index("tx")
        half_cols = width // halves
        pairs = [(0, 1), (1, 0)]
        other_weight = lax.ppermute(
            lax.dynamic_slice_in_dim(out_rows, (1 - core) * half_cols, half_cols, axis=1), "tx", pairs
        )
        own_weight = lax.dynamic_slice_in_dim(out_rows, core * half_cols, half_cols, axis=1)
        other_attended = lax.ppermute(attended, "tx", pairs)
        across_cores = jnp.dot(attended, own_weight, preferred_element_type=jnp.float32) + jnp.dot(
            other_attended, other_weight, preferred_element_type=jnp.float32
        )
    else:
        partial_value = jnp.dot(attended, out_rows, preferred_element_type=jnp.float32)
        across_cores = lax.psum_scatter(partial_value, "tx", scatter_dimension=1, tiled=True)
    mixed = lax.psum_scatter(
        across_cores.astype(jnp.bfloat16), "ty", scatter_dimension=1, tiled=True
    )
    return (mixed, new_cache)


def solution(mesh):
    return jax.shard_map(
        per_device,
        mesh=mesh,
        in_specs=(
            P("dp", "tx"),
            P(None, "ty", "tx"),
            P(None, "ty", None),
            P("ty", "tx", None),
            P("dp", "ty", None, None),
            P(),
            P(),
            P(),
        ),
        out_specs=(P("dp", ("tx", "ty")), P("dp", "ty", None, None)),
        check_vma=False,
    )
```

```python
import math

import jax
import jax.numpy as jnp
from jax import lax
from jax.sharding import PartitionSpec as P

HEAD_SIZE = 64
WINDOW_LENGTH = 2048


EPS = 1e-05


def apply_rotary(values, token_positions):
    width = values.shape[-1]
    half_width = width // 2
    freqs = jnp.exp(jnp.arange(half_width, dtype=jnp.float32) * (-2.0 * math.log(10000.0) / width))
    angles = token_positions.astype(jnp.float32)[:, None] * freqs[None, :]
    cosine = jnp.cos(angles)[:, None, :]
    sine = jnp.sin(angles)[:, None, :]
    leading = values[..., :half_width]
    trailing = values[..., half_width:]
    return jnp.concatenate(
        [leading * cosine - trailing * sine, trailing * cosine + leading * sine], axis=-1
    )


def carry_in(window):
    return lax.all_to_all(window, "dp", split_axis=0, concat_axis=0, tiled=True)


def carry_out(window):
    return lax.all_to_all(window, "dp", split_axis=0, concat_axis=0, tiled=True)


def reorder(window, order, groups):
    columns = window.shape[1]
    blocks = window.reshape(groups, window.shape[0] // groups, columns)
    return jnp.take(blocks, order, axis=0).reshape(window.shape[0], columns)


def per_device(
    tokens, query_weight, key_value_weight, output_weight, cache, lengths, offsets, slots
):
    request = lax.axis_index("dp")
    groups = lax.axis_size("dp")
    stored = cache[0, 0]
    half_rows = stored.shape[0]
    spread = carry_in(stored)
    whole = lax.all_gather(tokens, "tx", axis=1, tiled=True)
    rows_new = whole.shape[0]
    width = whole.shape[1]
    floats = whole.astype(jnp.float32)
    normalized_input = (
        floats * lax.rsqrt(jnp.mean(floats * floats, axis=1, keepdims=True) + EPS)
    ).astype(jnp.bfloat16)
    owners = jnp.arange(slots.shape[0], dtype=jnp.int32)
    inverse = jnp.sum(jnp.where(slots[None, :] == owners[:, None], owners[None, :], 0), axis=1)
    length = lengths[request]
    offset = offsets[request]
    token_positions = length + jnp.arange(rows_new, dtype=jnp.int32)
    rotation_pairs = jnp.dot(
        normalized_input,
        key_value_weight.reshape(width, 2 * HEAD_SIZE),
        preferred_element_type=jnp.float32,
    )
    new_keys = apply_rotary(rotation_pairs[:, None, :HEAD_SIZE], token_positions)[:, 0].astype(
        jnp.bfloat16
    )
    new_values = rotation_pairs[:, HEAD_SIZE:].astype(jnp.bfloat16)
    entry = jnp.concatenate([new_keys, new_values], axis=1)

    spread, entry = lax.optimization_barrier((spread, entry))
    window_chunk = half_rows // groups
    entry_chunk = rows_new // groups
    lanes = stored.shape[1]
    second = jnp.concatenate(
        [
            jnp.take(spread.reshape(groups, window_chunk, lanes), slots, axis=0, mode="clip"),
            entry.reshape(groups, entry_chunk, lanes),
        ],
        axis=1,
    ).reshape(groups * (window_chunk + entry_chunk), lanes)
    delivered = carry_in(second).reshape(groups, window_chunk + entry_chunk, lanes)
    window = delivered[:, :window_chunk].reshape(half_rows, lanes)
    entry_parts = delivered[:, window_chunk:]

    query_cols = query_weight.shape[2]
    heads = query_cols // HEAD_SIZE
    queries = jnp.dot(
        normalized_input,
        query_weight.reshape(width, query_cols),
        preferred_element_type=jnp.float32,
    )
    query_rotated = apply_rotary(
        queries.reshape(rows_new, heads, HEAD_SIZE), token_positions
    ).astype(jnp.bfloat16)
    factor = 1.0 / math.sqrt(HEAD_SIZE)
    rows = jnp.arange(rows_new, dtype=jnp.int32)
    new_mask = rows[None, :] <= rows[:, None]
    cycle = jnp.arange(WINDOW_LENGTH, dtype=jnp.int32)
    held = length - 1 - jnp.mod(offset - 1 - cycle, WINDOW_LENGTH)
    cache_mask = (held[None, :] >= 0) & (held[None, :] > token_positions[:, None] - WINDOW_LENGTH)
    window_keys = window[:, :HEAD_SIZE]
    window_values = window[:, HEAD_SIZE:]

    def one_head(query_rows):
        old_scores = (
            jnp.einsum("qd,kd->qk", query_rows, window_keys, preferred_element_type=jnp.float32)
            * factor
        )
        new_scores = (
            jnp.einsum("qd,kd->qk", query_rows, new_keys, preferred_element_type=jnp.float32)
            * factor
        )
        old_scores = jnp.where(cache_mask, old_scores, -jnp.inf)
        new_scores = jnp.where(new_mask, new_scores, -jnp.inf)
        top = jnp.maximum(
            jnp.max(old_scores, axis=1, keepdims=True), jnp.max(new_scores, axis=1, keepdims=True)
        )
        old_powers = jnp.exp(old_scores - top)
        new_powers = jnp.exp(new_scores - top)
        total = jnp.sum(old_powers, axis=1, keepdims=True) + jnp.sum(
            new_powers, axis=1, keepdims=True
        )
        summed = jnp.dot(
            old_powers.astype(jnp.bfloat16), window_values, preferred_element_type=jnp.float32
        ) + jnp.dot(new_powers.astype(jnp.bfloat16), new_values, preferred_element_type=jnp.float32)
        return (summed / total).astype(jnp.bfloat16)

    outputs = lax.map(one_head, jnp.transpose(query_rotated, (1, 0, 2)))
    attended = jnp.transpose(outputs, (1, 0, 2)).reshape(rows_new, heads * HEAD_SIZE)

    arrived = carry_out(jnp.take(entry_parts, inverse, axis=0, mode="clip").reshape(rows_new, lanes))
    own_offset = offsets[inverse[request]]
    extended = jnp.concatenate([stored, stored[:rows_new]], axis=0)
    extended = lax.dynamic_update_slice_in_dim(extended, arrived, own_offset, axis=0)
    wrap = own_offset + rows_new - WINDOW_LENGTH
    head_rows = jnp.arange(rows_new, dtype=jnp.int32)[:, None]
    head = jnp.where(head_rows < wrap, extended[WINDOW_LENGTH:], extended[:rows_new])
    updated = jnp.concatenate([head, extended[rows_new:WINDOW_LENGTH]], axis=0)
    new_cache = updated[None, None]
    out_rows = output_weight.reshape(output_weight.shape[1], width)
    halves = lax.axis_size("tx")
    if halves == 2:
        core = lax.axis_index("tx")
        half_cols = width // halves
        pairs = [(0, 1), (1, 0)]
        other_weight = lax.ppermute(
            lax.dynamic_slice_in_dim(out_rows, (1 - core) * half_cols, half_cols, axis=1), "tx", pairs
        )
        own_weight = lax.dynamic_slice_in_dim(out_rows, core * half_cols, half_cols, axis=1)
        other_attended = lax.ppermute(attended, "tx", pairs)
        across_cores = jnp.dot(attended, own_weight, preferred_element_type=jnp.float32) + jnp.dot(
            other_attended, other_weight, preferred_element_type=jnp.float32
        )
    else:
        partial_value = jnp.dot(attended, out_rows, preferred_element_type=jnp.float32)
        across_cores = lax.psum_scatter(partial_value, "tx", scatter_dimension=1, tiled=True)
    mixed = lax.psum_scatter(
        across_cores.astype(jnp.bfloat16), "ty", scatter_dimension=1, tiled=True
    )
    return (mixed, new_cache)


def solution(mesh):
    return jax.shard_map(
        per_device,
        mesh=mesh,
        in_specs=(
            P("dp", "tx"),
            P(None, "ty", "tx"),
            P(None, "ty", None),
            P("ty", "tx", None),
            P("dp", "ty", None, None),
            P(),
            P(),
            P(),
        ),
        out_specs=(P("dp", ("tx", "ty")), P("dp", "ty", None, None)),
        check_vma=False,
    )
```

```python
import math

import jax
import jax.numpy as jnp
from jax import lax
from jax.sharding import PartitionSpec as P

HEAD_SIZE = 64
WINDOW_LENGTH = 2048


EPS = 1e-05


def apply_rotary(values, token_positions):
    width = values.shape[-1]
    half_width = width // 2
    freqs = jnp.exp(jnp.arange(half_width, dtype=jnp.float32) * (-2.0 * math.log(10000.0) / width))
    angles = token_positions.astype(jnp.float32)[:, None] * freqs[None, :]
    cosine = jnp.cos(angles)[:, None, :]
    sine = jnp.sin(angles)[:, None, :]
    leading = values[..., :half_width]
    trailing = values[..., half_width:]
    return jnp.concatenate(
        [leading * cosine - trailing * sine, trailing * cosine + leading * sine], axis=-1
    )


def carry_in(window):
    return lax.all_to_all(window, "dp", split_axis=0, concat_axis=0, tiled=True)


def carry_out(window):
    return lax.all_to_all(window, "dp", split_axis=0, concat_axis=0, tiled=True)


def reorder(window, order, groups):
    columns = window.shape[1]
    blocks = window.reshape(groups, window.shape[0] // groups, columns)
    return jnp.take(blocks, order, axis=0).reshape(window.shape[0], columns)


def per_device(
    tokens, query_weight, key_value_weight, output_weight, cache, lengths, offsets, slots
):
    request = lax.axis_index("dp")
    groups = lax.axis_size("dp")
    stored = cache[0, 0]
    half_rows = stored.shape[0]
    spread = carry_in(stored)
    whole = lax.all_gather(tokens, "tx", axis=1, tiled=True)
    rows_new = whole.shape[0]
    width = whole.shape[1]
    floats = whole.astype(jnp.float32)
    normalized_input = (
        floats * lax.rsqrt(jnp.mean(floats * floats, axis=1, keepdims=True) + EPS)
    ).astype(jnp.bfloat16)
    owners = jnp.arange(slots.shape[0], dtype=jnp.int32)
    inverse = jnp.sum(jnp.where(slots[None, :] == owners[:, None], owners[None, :], 0), axis=1)
    length = lengths[request]
    offset = offsets[request]
    token_positions = length + jnp.arange(rows_new, dtype=jnp.int32)
    rotation_pairs = jnp.dot(
        normalized_input,
        key_value_weight.reshape(width, 2 * HEAD_SIZE),
        preferred_element_type=jnp.float32,
    )
    new_keys = apply_rotary(rotation_pairs[:, None, :HEAD_SIZE], token_positions)[:, 0].astype(
        jnp.bfloat16
    )
    new_values = rotation_pairs[:, HEAD_SIZE:].astype(jnp.bfloat16)
    entry = jnp.concatenate([new_keys, new_values], axis=1)

    spread, entry = lax.optimization_barrier((spread, entry))
    window_chunk = half_rows // groups
    entry_chunk = rows_new // groups
    lanes = stored.shape[1]
    second = jnp.concatenate(
        [
            jnp.take(spread.reshape(groups, window_chunk, lanes), slots, axis=0, mode="clip"),
            entry.reshape(groups, entry_chunk, lanes),
        ],
        axis=1,
    ).reshape(groups * (window_chunk + entry_chunk), lanes)
    delivered = carry_in(second).reshape(groups, window_chunk + entry_chunk, lanes)
    window = delivered[:, :window_chunk].reshape(half_rows, lanes)
    entry_parts = delivered[:, window_chunk:]

    query_cols = query_weight.shape[2]
    heads = query_cols // HEAD_SIZE
    queries = jnp.dot(
        normalized_input,
        query_weight.reshape(width, query_cols),
        preferred_element_type=jnp.float32,
    )
    query_rotated = apply_rotary(
        queries.reshape(rows_new, heads, HEAD_SIZE), token_positions
    ).astype(jnp.bfloat16)
    factor = 1.0 / math.sqrt(HEAD_SIZE)
    rows = jnp.arange(rows_new, dtype=jnp.int32)
    new_mask = rows[None, :] <= rows[:, None]
    cycle = jnp.arange(WINDOW_LENGTH, dtype=jnp.int32)
    held = length - 1 - jnp.mod(offset - 1 - cycle, WINDOW_LENGTH)
    cache_mask = (held[None, :] >= 0) & (held[None, :] > token_positions[:, None] - WINDOW_LENGTH)
    window_keys = window[:, :HEAD_SIZE]
    window_values = window[:, HEAD_SIZE:]

    def one_head(query_rows):
        old_scores = (
            jnp.einsum("qd,kd->qk", query_rows, window_keys, preferred_element_type=jnp.float32)
            * factor
        )
        new_scores = (
            jnp.einsum("qd,kd->qk", query_rows, new_keys, preferred_element_type=jnp.float32)
            * factor
        )
        old_scores = jnp.where(cache_mask, old_scores, -jnp.inf)
        new_scores = jnp.where(new_mask, new_scores, -jnp.inf)
        top = jnp.maximum(
            jnp.max(old_scores, axis=1, keepdims=True), jnp.max(new_scores, axis=1, keepdims=True)
        )
        old_powers = jnp.exp(old_scores - top)
        new_powers = jnp.exp(new_scores - top)
        total = jnp.sum(old_powers, axis=1, keepdims=True) + jnp.sum(
            new_powers, axis=1, keepdims=True
        )
        summed = jnp.dot(
            old_powers.astype(jnp.bfloat16), window_values, preferred_element_type=jnp.float32
        ) + jnp.dot(new_powers.astype(jnp.bfloat16), new_values, preferred_element_type=jnp.float32)
        return (summed / total).astype(jnp.bfloat16)

    outputs = lax.map(one_head, jnp.transpose(query_rotated, (1, 0, 2)))
    attended = jnp.transpose(outputs, (1, 0, 2)).reshape(rows_new, heads * HEAD_SIZE)

    arrived = carry_out(jnp.take(entry_parts, inverse, axis=0, mode="clip").reshape(rows_new, lanes))
    own_offset = offsets[inverse[request]]
    padded = jnp.concatenate(
        [arrived, jnp.zeros((stored.shape[0] - rows_new, lanes), arrived.dtype)], axis=0
    )
    placed = jnp.roll(padded, own_offset, axis=0)
    slot_rows = jnp.arange(stored.shape[0], dtype=jnp.int32)[:, None]
    fresh = jnp.mod(slot_rows - own_offset, WINDOW_LENGTH) < rows_new
    updated = jnp.where(fresh, placed, stored)
    new_cache = updated[None, None]
    out_rows = output_weight.reshape(output_weight.shape[1], width)
    halves = lax.axis_size("tx")
    if halves == 2:
        core = lax.axis_index("tx")
        half_cols = width // halves
        pairs = [(0, 1), (1, 0)]
        other_weight = lax.ppermute(
            lax.dynamic_slice_in_dim(out_rows, (1 - core) * half_cols, half_cols, axis=1), "tx", pairs
        )
        own_weight = lax.dynamic_slice_in_dim(out_rows, core * half_cols, half_cols, axis=1)
        other_attended = lax.ppermute(attended, "tx", pairs)
        across_cores = jnp.dot(attended, own_weight, preferred_element_type=jnp.float32) + jnp.dot(
            other_attended, other_weight, preferred_element_type=jnp.float32
        )
    else:
        partial_value = jnp.dot(attended, out_rows, preferred_element_type=jnp.float32)
        across_cores = lax.psum_scatter(partial_value, "tx", scatter_dimension=1, tiled=True)
    mixed = lax.psum_scatter(
        across_cores.astype(jnp.bfloat16), "ty", scatter_dimension=1, tiled=True
    )
    return (mixed, new_cache)


def solution(mesh):
    return jax.shard_map(
        per_device,
        mesh=mesh,
        in_specs=(
            P("dp", "tx"),
            P(None, "ty", "tx"),
            P(None, "ty", None),
            P("ty", "tx", None),
            P("dp", "ty", None, None),
            P(),
            P(),
            P(),
        ),
        out_specs=(P("dp", ("tx", "ty")), P("dp", "ty", None, None)),
        check_vma=False,
    )
```
